128 devices in a mesh: sky: 16 (over x, y), gz: 8 (over z, core).
Axes of the slice: x: 4, y: 4, z: 4, core: 2. Of those that a mesh axis runs over, the one named last changes fastest.
Arguments:
- spectra: bfloat16 [4096, 1032], P('sky', 'gz'), may hold values from -6 to 6
- kernel: bfloat16 [4096, 16], P('sky'), may hold values from 0.049804688 to 0.59765625
- owner: int32 [4096, 1], P('sky'), may hold values from 0 to 15; in each aligned block of 256 rows (0 to 255, 256 to 511, ...) at most 20 rows name the same one
- offset: int32 [4096], P('sky'), may hold values from 0 to 4095
Outputs:
- spectrum: float32 [2, 256, 256, 1032], P(None, None, ('sky', 'gz'))
The draws below stay inside these ranges and needn't reach their ends.
Inputs may be any that keep to these rules, and one draw needn't show every extreme that they name: `owner`: in each aligned block of 256 rows no sky index is named by more than 20 rows, a bound that some block reaches.
All inputs are finite; a program needn't handle non-finite values.
Results may differ from the reference program's by a relative error of at most 0.0063.
Values may be sent and summed in bfloat16 or wider, within the bound.
No kernel may reach another device: no remote copies, remote signals or barrier semaphores. Data moves between devices by JAX's collectives and lax.ppermute only.
A program may use at most 64 MiB of HBM per device.

```python
import math
import jax
import jax.numpy as jnp
import numpy as np

NX = 256
NY = 256
NW = 1032
KSIDE = 4
FIB_DEV = 256
FIBRES = 4096
N_SKY = 16


def set_ends(array, rng, smallest, largest):
    shape = array.shape
    spot = [jax.random.randint(jax.random.fold_in(rng, axis), (), 0, shape[axis]) for axis in range(len(shape))]
    array = array.at[tuple(spot)].set(smallest)
    longest = shape.index(max(shape))
    spot[longest] = (spot[longest] + 1) % shape[longest]
    return array.at[tuple(spot)].set(largest)


def level_of(key, shape, shards, low, largest):
    gain = 1.0
    for axis_at, blocks in shards:
        draws = jax.random.uniform(jax.random.fold_in(jax.random.fold_in(key, 6), axis_at), (blocks,), jnp.float32, low / len(shards), largest / len(shards))
        gain = gain * jnp.repeat(jnp.exp(draws), shape[axis_at] // blocks).reshape((-1,) + (1,) * (len(shape) - 1 - axis_at))
    return gain


def shared_out(stream_key, own, number, rows, count, top, most, skew):
    order = jax.random.permutation(stream_key, count)
    heavy_load, ordinary = load_shares(count, rows * top, most, skew, True), load_shares(count, rows * top, most, skew, False)
    places = jnp.arange(count)

    def named(tallies, rotation):
        used = int((tallies > 0).sum())
        fixed = max(1, used // 4)
        moved = fixed + (places - fixed + rotation * (used - fixed)) % max(1, count - fixed)
        return jnp.zeros((count,), jnp.int32).at[order[jnp.where(places < fixed, places, moved)]].set(jnp.asarray(tallies, jnp.int32))

    tallies = jnp.where(number % 4 == 0, named(heavy_load, number // 4), named(ordinary, number - number // 4 - 1))
    mixed = jax.random.permutation(jax.random.fold_in(own, 3), count)
    source_of, sink = mixed[0:count // 2 * 2:2], mixed[1:count // 2 * 2:2]
    room = jnp.minimum(tallies[source_of] - 1, most - tallies[sink]) // 2
    room = jnp.where((source_of == order[0]) | (sink == order[0]) | (tallies[sink] == 0), 0, jnp.maximum(room, 0))
    moved = jax.random.randint(jax.random.fold_in(own, 4), (count // 2,), 0, 1 << 20) % (room + 1)
    tallies = tallies.at[source_of].add(-moved).at[sink].add(moved)
    members = jnp.searchsorted(jnp.cumsum(tallies), jnp.arange(rows * top), side="right").astype(jnp.int32)
    grid = members.reshape(top, rows).T
    grid = grid[jax.random.permutation(jax.random.fold_in(own, 1), rows)]
    rotation = jax.random.randint(jax.random.fold_in(own, 2), (rows, 1), 0, top)
    return jnp.take_along_axis(grid, (jnp.arange(top)[None, :] + rotation) % top, axis=1)


def load_shares(count, total, bound, lean, full):
    portions = [(1 << 20) // math.isqrt(rank ** lean) + 1 for rank in range(1, count + 1)]
    largest = bound if full else min(bound, max(-(-total // count), total * portions[0] // sum(portions)))
    least = 1 if total - largest >= count - 1 else 0
    given, surplus = [largest] + [least] * (count - 1), total - largest - least * (count - 1)
    while surplus > 0:
        candidates = [i for i in range(1, count) if given[i] < largest] or [i for i in range(1, count) if given[i] < bound]
        pool, budget = sum([portions[i] for i in candidates]), surplus
        for i in candidates:
            more = min(bound - given[i], max(1, budget * portions[i] // pool), surplus)
            given[i] = given[i] + more
            surplus = surplus - more
    return np.array(given)


def normal_values(stream_key, dims, scale, reach, pieces=(), held_as=jnp.bfloat16):
    level = level_of(stream_key, dims, pieces, -0.22, 0.18) if pieces else 1.0
    drawn = jax.random.normal(stream_key, dims, jnp.float32) * scale * level
    return jnp.minimum(jnp.maximum(drawn, -reach), reach).astype(held_as)


def setup_inputs(seed: int = 0) -> dict:
    arg_keys = jax.random.split(jax.random.key(seed), 5)
    spectra = normal_values(arg_keys[0], (FIBRES, NW), 1.0, 6.0, ((0, 16), (1, 8)))
    kernel = jnp.clip(0.049804688 + 0.54785156 * jax.random.uniform(arg_keys[1], (FIBRES, KSIDE * KSIDE), jnp.float32) ** level_of(arg_keys[1], (FIBRES, KSIDE * KSIDE), ((0, 16),), -0.2, 0.2), 0.049804688, 0.59765625).astype(jnp.bfloat16)
    owner_keys = jax.random.split(jax.random.fold_in(arg_keys[2], 1), FIBRES // FIB_DEV)
    owner_turns = jax.random.permutation(jax.random.fold_in(arg_keys[2], 3), FIBRES // FIB_DEV)
    owner = jax.vmap(lambda own, number: shared_out(jax.random.fold_in(arg_keys[2], 2), own, number, FIB_DEV, N_SKY, 1, FIB_DEV * 5 // (4 * N_SKY), 2))(owner_keys, owner_turns).reshape((FIBRES, 1))
    offset = set_ends(jax.random.randint(arg_keys[3], (FIBRES,), 0, (NX // N_SKY) * NY), jax.random.fold_in(arg_keys[3], 1), 0, ((NX // N_SKY) * NY) - 1).astype(jnp.int32)
    return dict(spectra=spectra, kernel=kernel, owner=owner, offset=offset)


def dft_tables(length):
    steps = jnp.arange(length, dtype=jnp.int32)
    phase = steps[:, None] * steps[None, :] % length
    angles = phase.astype(jnp.float32) * (2.0 * math.pi / length)
    factor = 1.0 / math.sqrt(length)
    return ((jnp.cos(angles) * factor).astype(jnp.bfloat16), (jnp.sin(angles) * factor).astype(jnp.bfloat16))

def reference(spectra, kernel, owner, offset):
    tile_rows = NX // N_SKY
    corner_row = owner[:, 0] * tile_rows + offset // NY
    corner_col = offset % NY
    values = spectra.astype(jnp.float32)
    weights = kernel.astype(jnp.float32)
    flat = jnp.zeros((NX * NY, NW), jnp.float32)
    for step_a in range(KSIDE):
        for step_b in range(KSIDE):
            target = (corner_row + step_a) % NX * NY + (corner_col + step_b) % NY
            flat = flat.at[target.astype(jnp.int32)].add(weights[:, step_a * KSIDE + step_b][:, None] * values)
    cube = flat.reshape(NX, NY, NW).astype(jnp.bfloat16).astype(jnp.float32)
    cos_y, sin_y = dft_tables(NY)
    first_re = jnp.einsum('xyw,yk->xkw', cube, cos_y.astype(jnp.float32)).astype(jnp.bfloat16).astype(jnp.float32)
    first_im = (-jnp.einsum('xyw,yk->xkw', cube, sin_y.astype(jnp.float32))).astype(jnp.bfloat16).astype(jnp.float32)
    cos_w, sin_w = dft_tables(NW)
    cos_w = cos_w.astype(jnp.float32)
    sin_w = sin_w.astype(jnp.float32)
    second_re = (jnp.einsum('xkw,wv->xkv', first_re, cos_w) + jnp.einsum('xkw,wv->xkv', first_im, sin_w)).astype(jnp.bfloat16).astype(jnp.float32)
    second_im = (jnp.einsum('xkw,wv->xkv', first_im, cos_w) - jnp.einsum('xkw,wv->xkv', first_re, sin_w)).astype(jnp.bfloat16).astype(jnp.float32)
    cos_x, sin_x = dft_tables(NX)
    cos_x = cos_x.astype(jnp.float32)
    sin_x = sin_x.astype(jnp.float32)
    third_re = jnp.einsum('xkv,xu->ukv', second_re, cos_x) + jnp.einsum('xkv,xu->ukv', second_im, sin_x)
    third_im = jnp.einsum('xkv,xu->ukv', second_im, cos_x) - jnp.einsum('xkv,xu->ukv', second_re, sin_x)
    return jnp.stack([third_re, third_im])
```

```python
import math

import jax
import jax.numpy as jnp
from jax import lax
from jax.sharding import PartitionSpec as P

NX = 256
NY = 256
NW = 1032
KSIDE = 4


def dft_tables(length):
    steps = jnp.arange(length, dtype=jnp.int32)
    phase = steps[:, None] * steps[None, :] % length
    angles = phase.astype(jnp.float32) * (2.0 * math.pi / length)
    factor = 1.0 / math.sqrt(length)
    return (
        (jnp.cos(angles) * factor).astype(jnp.bfloat16),
        (jnp.sin(angles) * factor).astype(jnp.bfloat16),
    )


def complex_table(length):
    cos_t, sin_t = dft_tables(length)
    top = jnp.concatenate([cos_t, -sin_t], axis=1)
    bottom = jnp.concatenate([sin_t, cos_t], axis=1)
    return jnp.concatenate([top, bottom], axis=0).reshape(2, length, 2, length)


def route_fibres(spectra, kernel, owner, offset, sky_count):
    fibre_count = spectra.shape[0]
    capacity = fibre_count * 5 // (4 * sky_count)
    block = 2 * capacity
    slots_all = sky_count * block
    target = owner[:, 0]
    order = jnp.arange(fibre_count, dtype=jnp.int32)
    same = (target[:, None] == target[None, :]) & (order[None, :] < order[:, None])
    before = jnp.sum(same.astype(jnp.int32), axis=1)
    first_slot = target * block + before
    second_slot = ((target + 1) % sky_count) * block + capacity + before
    slot_ids = jnp.arange(slots_all, dtype=jnp.int32)
    pick = (
        (slot_ids[:, None] == first_slot[None, :]) | (slot_ids[:, None] == second_slot[None, :])
    ).astype(jnp.bfloat16)
    row = (offset // NY).astype(jnp.bfloat16)[:, None]
    col = (offset % NY).astype(jnp.bfloat16)[:, None]
    packed = jnp.concatenate([spectra, kernel, row, col], axis=1)
    send = jnp.dot(pick, packed, preferred_element_type=jnp.float32).astype(jnp.bfloat16)
    send = send.reshape(sky_count, block, packed.shape[1])
    got = lax.all_to_all(send, "sky", split_axis=0, concat_axis=0, tiled=True)
    return got.reshape(slots_all, packed.shape[1]), capacity, block


def grid_tile(got, slab_width, taps, tile_rows, capacity, block):
    slots_all = got.shape[0]
    values = got[:, :slab_width]
    weights = got[:, slab_width : slab_width + taps].astype(jnp.float32)
    slot_ids = jnp.arange(slots_all, dtype=jnp.int32)
    shift = jnp.where(slot_ids % block >= capacity, tile_rows, 0)
    corner_row = got[:, slab_width + taps].astype(jnp.int32) - shift
    corner_col = got[:, slab_width + taps + 1].astype(jnp.int32)
    rows = jnp.arange(tile_rows, dtype=jnp.int32)
    columns = jnp.arange(NY, dtype=jnp.int32)
    spread = jnp.zeros((slots_all, tile_rows, NY), jnp.float32)
    for step_a in range(KSIDE):
        active = rows[None, :] == (corner_row + step_a)[:, None]
        line = jnp.zeros((slots_all, NY), jnp.float32)
        for step_b in range(KSIDE):
            placed = columns[None, :] == ((corner_col + step_b) % NY)[:, None]
            line = line + jnp.where(placed, weights[:, step_a * KSIDE + step_b][:, None], 0.0)
        spread = spread + jnp.where(active[:, :, None], line[:, None, :], 0.0)
    spread_bf = spread.astype(jnp.bfloat16).reshape(slots_all, tile_rows * NY)
    cube = lax.dot_general(
        spread_bf, values, (((0,), (0,)), ((), ())), preferred_element_type=jnp.float32
    )
    return cube.astype(jnp.bfloat16).reshape(tile_rows, NY, slab_width)


def shards(spectra, kernel, owner, offset):
    sky_count = lax.axis_size("sky")
    gz_count = lax.axis_size("gz")
    devices = sky_count * gz_count
    slab_width = spectra.shape[1]
    taps = kernel.shape[1]
    tile_rows = NX // sky_count
    per_dev = NY // devices

    got, capacity, block = route_fibres(spectra, kernel, owner, offset, sky_count)
    cube_bf = grid_tile(got, slab_width, taps, tile_rows, capacity, block)

    cos_y, sin_y = dft_tables(NY)
    table_y = jnp.concatenate([cos_y, -sin_y], axis=1).reshape(NY, 2, devices, per_dev)
    table_w = complex_table(NW).reshape(2, gz_count, slab_width, 2, NW)
    table_x = complex_table(NX).reshape(2, sky_count, tile_rows, 2, NX)
    table_y, table_w, table_x = lax.optimization_barrier((table_y, table_w, table_x))

    first = jnp.einsum(
        "xyw,yrdk->dxrkw", cube_bf, table_y, preferred_element_type=jnp.float32
    ).astype(jnp.bfloat16)
    gathered = lax.all_to_all(first, ("sky", "gz"), split_axis=0, concat_axis=0, tiled=True)
    gathered = gathered.reshape(sky_count, gz_count, tile_rows, 2, per_dev, slab_width)
    second = jnp.einsum(
        "sgxrkw,rgwRv->Rsxkv", gathered, table_w, preferred_element_type=jnp.float32
    ).astype(jnp.bfloat16)
    return jnp.einsum("Rsxkv,RsxUu->Uukv", second, table_x, preferred_element_type=jnp.float32)


def solution(mesh):
    in_specs = (P("sky", "gz"), P("sky", None), P("sky", None), P("sky"))
    out_specs = P(None, None, ("sky", "gz"), None)
    return jax.shard_map(shards, mesh=mesh, in_specs=in_specs, out_specs=out_specs, check_vma=False)
```

```python
import math

import jax
import jax.numpy as jnp
from jax import lax
from jax.sharding import PartitionSpec as P

NX = 256
NY = 256
NW = 1032
KSIDE = 4


def dft_tables(length):
    steps = jnp.arange(length, dtype=jnp.int32)
    phase = steps[:, None] * steps[None, :] % length
    angles = phase.astype(jnp.float32) * (2.0 * math.pi / length)
    factor = 1.0 / math.sqrt(length)
    return (
        (jnp.cos(angles) * factor).astype(jnp.bfloat16),
        (jnp.sin(angles) * factor).astype(jnp.bfloat16),
    )


def twiddles(length):
    q = math.isqrt(length - 1) + 1
    coarse_count = -(-length // q)
    steps = jnp.arange(length, dtype=jnp.int32)
    angle = 2.0 * math.pi / length
    coarse = (jnp.arange(coarse_count, dtype=jnp.int32)[:, None] * q * steps[None, :]) % length
    fine = (jnp.arange(q, dtype=jnp.int32)[:, None] * steps[None, :]) % length
    cos_c = jnp.cos(coarse.astype(jnp.float32) * angle)[:, None, :]
    sin_c = jnp.sin(coarse.astype(jnp.float32) * angle)[:, None, :]
    cos_f = jnp.cos(fine.astype(jnp.float32) * angle)[None, :, :]
    sin_f = jnp.sin(fine.astype(jnp.float32) * angle)[None, :, :]
    cos_t = (cos_c * cos_f - sin_c * sin_f).reshape(coarse_count * q, length)[:length]
    sin_t = (sin_c * cos_f + cos_c * sin_f).reshape(coarse_count * q, length)[:length]
    return cos_t, sin_t


def complex_table(length, cos_sin=None):
    if cos_sin is None:
        cos_t, sin_t = dft_tables(length)
    else:
        factor = 1.0 / math.sqrt(length)
        cos_t = (cos_sin[0] * factor).astype(jnp.bfloat16)
        sin_t = (cos_sin[1] * factor).astype(jnp.bfloat16)
    top = jnp.concatenate([cos_t, -sin_t], axis=1)
    bottom = jnp.concatenate([sin_t, cos_t], axis=1)
    return jnp.concatenate([top, bottom], axis=0)


def route_fibres(spectra, kernel, owner, offset, sky_count):
    fibre_count = spectra.shape[0]
    capacity = fibre_count * 5 // (4 * sky_count)
    block = 2 * capacity
    slots_all = sky_count * block
    target = owner[:, 0]
    order = jnp.arange(fibre_count, dtype=jnp.int32)
    same = (target[:, None] == target[None, :]) & (order[None, :] < order[:, None])
    before = jnp.sum(same.astype(jnp.int32), axis=1)
    first_slot = target * block + before
    second_slot = ((target + 1) % sky_count) * block + capacity + before
    slot_ids = jnp.arange(slots_all, dtype=jnp.int32)
    pick = (
        (slot_ids[:, None] == first_slot[None, :]) | (slot_ids[:, None] == second_slot[None, :])
    ).astype(jnp.bfloat16)
    row = (offset // NY).astype(jnp.bfloat16)[:, None]
    col = (offset % NY).astype(jnp.bfloat16)[:, None]
    packed = jnp.concatenate([spectra, kernel, row, col], axis=1)
    send = jnp.dot(pick, packed, preferred_element_type=jnp.float32).astype(jnp.bfloat16)
    send = send.reshape(sky_count, block * packed.shape[1])
    got = lax.all_to_all(send, "sky", split_axis=0, concat_axis=0, tiled=True)
    return got.reshape(slots_all, packed.shape[1]), capacity, block


def grid_tile(got, slab_width, taps, tile_rows, capacity, block):
    slots_all = got.shape[0]
    values = got[:, :slab_width]
    weights = got[:, slab_width : slab_width + taps].astype(jnp.float32)
    slot_ids = jnp.arange(slots_all, dtype=jnp.int32)
    shift = jnp.where(slot_ids % block >= capacity, tile_rows, 0)
    corner_row = got[:, slab_width + taps].astype(jnp.int32) - shift
    corner_col = got[:, slab_width + taps + 1].astype(jnp.int32)
    rows = jnp.arange(tile_rows, dtype=jnp.int32)
    columns = jnp.arange(NY, dtype=jnp.int32)
    spread = jnp.zeros((slots_all, tile_rows, NY), jnp.float32)
    for step_a in range(KSIDE):
        active = rows[None, :] == (corner_row + step_a)[:, None]
        line = jnp.zeros((slots_all, NY), jnp.float32)
        for step_b in range(KSIDE):
            placed = columns[None, :] == ((corner_col + step_b) % NY)[:, None]
            line = line + jnp.where(placed, weights[:, step_a * KSIDE + step_b][:, None], 0.0)
        spread = spread + jnp.where(active[:, :, None], line[:, None, :], 0.0)
    spread_bf = spread.astype(jnp.bfloat16).reshape(slots_all, tile_rows * NY)
    cube = lax.dot_general(
        spread_bf, values, (((0,), (0,)), ((), ())), preferred_element_type=jnp.float32
    )
    return cube.astype(jnp.bfloat16).reshape(tile_rows, NY, slab_width)


def shards(spectra, kernel, owner, offset):
    sky_count = lax.axis_size("sky")
    gz_count = lax.axis_size("gz")
    devices = sky_count * gz_count
    slab_width = spectra.shape[1]
    taps = kernel.shape[1]
    tile_rows = NX // sky_count
    per_dev = NY // devices

    got, capacity, block = route_fibres(spectra, kernel, owner, offset, sky_count)
    cube_bf = grid_tile(got, slab_width, taps, tile_rows, capacity, block)

    cos_y, sin_y = dft_tables(NY)
    table_y = jnp.concatenate([cos_y, -sin_y], axis=1).reshape(NY, 2, devices, per_dev)
    table_w = complex_table(NW, twiddles(NW))
    table_x = complex_table(NX).reshape(2, sky_count, tile_rows, 2, NX)
    table_y, table_w, table_x = lax.optimization_barrier((table_y, table_w, table_x))

    first = jnp.einsum(
        "xyw,yrdk->dxrkw", cube_bf, table_y, preferred_element_type=jnp.float32
    ).astype(jnp.bfloat16)
    first = first.reshape(devices, tile_rows * 2 * per_dev * slab_width)
    gathered = lax.all_to_all(first, ("sky", "gz"), split_axis=0, concat_axis=0, tiled=True)
    gathered = gathered.reshape(sky_count, gz_count, tile_rows, 2, per_dev, slab_width)
    rows_w = jnp.transpose(gathered, (4, 0, 2, 3, 1, 5)).reshape(per_dev * NX, 2 * NW)
    second = jnp.dot(rows_w, table_w, preferred_element_type=jnp.float32).astype(jnp.bfloat16)
    second = second.reshape(per_dev, sky_count, tile_rows, 2, NW)
    return jnp.einsum("ksxRv,RsxUu->Uukv", second, table_x, preferred_element_type=jnp.float32)


def solution(mesh):
    in_specs = (P("sky", "gz"), P("sky", None), P("sky", None), P("sky"))
    out_specs = P(None, None, ("sky", "gz"), None)
    return jax.shard_map(shards, mesh=mesh, in_specs=in_specs, out_specs=out_specs, check_vma=False)
```

```python
import math

import jax
import jax.numpy as jnp
from jax import lax
from jax.sharding import PartitionSpec as P

NX = 256
NY = 256
NW = 1032
KSIDE = 4


def dft_tables(length):
    steps = jnp.arange(length, dtype=jnp.int32)
    phase = steps[:, None] * steps[None, :] % length
    angles = phase.astype(jnp.float32) * (2.0 * math.pi / length)
    factor = 1.0 / math.sqrt(length)
    return (
        (jnp.cos(angles) * factor).astype(jnp.bfloat16),
        (jnp.sin(angles) * factor).astype(jnp.bfloat16),
    )


def twiddles(length, fine_count=16):
    coarse_count = -(-length // fine_count)
    steps = jnp.arange(length, dtype=jnp.int32)
    angle = 2.0 * math.pi / length
    coarse = (jnp.arange(coarse_count, dtype=jnp.int32)[:, None] * fine_count * steps[None, :]) % length
    fine = (jnp.arange(fine_count, dtype=jnp.int32)[:, None] * steps[None, :]) % length
    cos_c = jnp.cos(coarse.astype(jnp.float32) * angle)[:, None, :]
    sin_c = jnp.sin(coarse.astype(jnp.float32) * angle)[:, None, :]
    cos_f = jnp.cos(fine.astype(jnp.float32) * angle)[None, :, :]
    sin_f = jnp.sin(fine.astype(jnp.float32) * angle)[None, :, :]
    rows = coarse_count * fine_count
    cos_t = (cos_c * cos_f - sin_c * sin_f).reshape(rows, length)[:length]
    sin_t = (sin_c * cos_f + cos_c * sin_f).reshape(rows, length)[:length]
    factor = 1.0 / math.sqrt(length)
    return (cos_t * factor).astype(jnp.bfloat16), (sin_t * factor).astype(jnp.bfloat16)


def complex_table(length):
    cos_t, sin_t = dft_tables(length)
    top = jnp.concatenate([cos_t, -sin_t], axis=1)
    bottom = jnp.concatenate([sin_t, cos_t], axis=1)
    return jnp.concatenate([top, bottom], axis=0)


def route_fibres(spectra, kernel, owner, offset, sky_count):
    fibre_count = spectra.shape[0]
    capacity = fibre_count * 5 // (4 * sky_count)
    block = 2 * capacity
    slots_all = sky_count * block
    target = owner[:, 0]
    order = jnp.arange(fibre_count, dtype=jnp.int32)
    same = (target[:, None] == target[None, :]) & (order[None, :] < order[:, None])
    before = jnp.sum(same.astype(jnp.int32), axis=1)
    first_slot = target * block + before
    second_slot = ((target + 1) % sky_count) * block + capacity + before
    slot_ids = jnp.arange(slots_all, dtype=jnp.int32)
    pick = (
        (slot_ids[:, None] == first_slot[None, :]) | (slot_ids[:, None] == second_slot[None, :])
    ).astype(jnp.bfloat16)
    row = (offset // NY).astype(jnp.bfloat16)[:, None]
    col = (offset % NY).astype(jnp.bfloat16)[:, None]
    packed = jnp.concatenate([spectra, kernel, row, col], axis=1)
    send = jnp.dot(pick, packed, preferred_element_type=jnp.float32).astype(jnp.bfloat16)
    send = send.reshape(sky_count, block * packed.shape[1])
    got = lax.all_to_all(send, "sky", split_axis=0, concat_axis=0, tiled=True)
    return got.reshape(slots_all, packed.shape[1]), capacity, block


def grid_tile(got, slab_width, taps, tile_rows, capacity, block):
    slots_all = got.shape[0]
    values = got[:, :slab_width]
    weights = got[:, slab_width : slab_width + taps].astype(jnp.float32)
    slot_ids = jnp.arange(slots_all, dtype=jnp.int32)
    shift = jnp.where(slot_ids % block >= capacity, tile_rows, 0)
    corner_row = got[:, slab_width + taps].astype(jnp.int32) - shift
    corner_col = got[:, slab_width + taps + 1].astype(jnp.int32)
    rows = jnp.arange(tile_rows, dtype=jnp.int32)
    columns = jnp.arange(NY, dtype=jnp.int32)
    spread = jnp.zeros((slots_all, tile_rows, NY), jnp.float32)
    for step_a in range(KSIDE):
        active = rows[None, :] == (corner_row + step_a)[:, None]
        line = jnp.zeros((slots_all, NY), jnp.float32)
        for step_b in range(KSIDE):
            placed = columns[None, :] == ((corner_col + step_b) % NY)[:, None]
            line = line + jnp.where(placed, weights[:, step_a * KSIDE + step_b][:, None], 0.0)
        spread = spread + jnp.where(active[:, :, None], line[:, None, :], 0.0)
    spread_bf = spread.astype(jnp.bfloat16).reshape(slots_all, tile_rows * NY)
    cube_t = lax.dot_general(
        values, spread_bf, (((0,), (0,)), ((), ())), preferred_element_type=jnp.float32
    )
    return cube_t.astype(jnp.bfloat16)


def shards(spectra, kernel, owner, offset):
    sky_count = lax.axis_size("sky")
    gz_count = lax.axis_size("gz")
    devices = sky_count * gz_count
    slab_width = spectra.shape[1]
    taps = kernel.shape[1]
    tile_rows = NX // sky_count
    per_dev = NY // devices

    got, capacity, block = route_fibres(spectra, kernel, owner, offset, sky_count)
    cube_t = grid_tile(got, slab_width, taps, tile_rows, capacity, block)
    cube_w = lax.all_to_all(cube_t, "gz", split_axis=1, concat_axis=0, tiled=True)
    rows_dev = tile_rows // gz_count
    cube_w = cube_w.reshape(NW, rows_dev, NY)

    cos_y, sin_y = dft_tables(NY)
    table_y = jnp.concatenate([cos_y, -sin_y], axis=1)
    cos_w, sin_w = twiddles(NW)
    table_x = complex_table(NX).reshape(2, devices, rows_dev, 2, NX)
    table_y, cos_w, sin_w, table_x = lax.optimization_barrier((table_y, cos_w, sin_w, table_x))

    first = jnp.einsum("wxy,yK->wxK", cube_w, table_y, preferred_element_type=jnp.float32)
    first = first.astype(jnp.bfloat16).reshape(NW, rows_dev, 2, NY)
    by_cos = jnp.einsum("wxrk,wv->rkxv", first, cos_w, preferred_element_type=jnp.float32)
    by_sin = jnp.einsum("wxrk,wv->rkxv", first, sin_w, preferred_element_type=jnp.float32)
    second = jnp.stack([by_cos[0] + by_sin[1], by_cos[1] - by_sin[0]], axis=2)
    second = second.astype(jnp.bfloat16).reshape(devices, per_dev * rows_dev * 2, NW)
    pencils = lax.all_to_all(second, ("sky", "gz"), split_axis=0, concat_axis=0, tiled=True)
    pencils = pencils.reshape(devices, per_dev, rows_dev, 2, NW)
    return jnp.einsum("sqxRv,RsxUu->Uuqv", pencils, table_x, preferred_element_type=jnp.float32)


def solution(mesh):
    in_specs = (P("sky", "gz"), P("sky", None), P("sky", None), P("sky"))
    out_specs = P(None, None, ("sky", "gz"), None)
    return jax.shard_map(shards, mesh=mesh, in_specs=in_specs, out_specs=out_specs, check_vma=False)
```

```python
import math

import jax
import jax.numpy as jnp
from jax import lax
from jax.sharding import PartitionSpec as P

NX = 256
NY = 256
NW = 1032
KSIDE = 4


def dft_tables(length):
    steps = jnp.arange(length, dtype=jnp.int32)
    phase = steps[:, None] * steps[None, :] % length
    angles = phase.astype(jnp.float32) * (2.0 * math.pi / length)
    factor = 1.0 / math.sqrt(length)
    return (
        (jnp.cos(angles) * factor).astype(jnp.bfloat16),
        (jnp.sin(angles) * factor).astype(jnp.bfloat16),
    )


def twiddles(length, fine_count=16):
    coarse_count = -(-length // fine_count)
    steps = jnp.arange(length, dtype=jnp.int32)
    angle = 2.0 * math.pi / length
    coarse = (jnp.arange(coarse_count, dtype=jnp.int32)[:, None] * fine_count * steps[None, :]) % length
    fine = (jnp.arange(fine_count, dtype=jnp.int32)[:, None] * steps[None, :]) % length
    cos_c = jnp.cos(coarse.astype(jnp.float32) * angle)[:, None, :]
    sin_c = jnp.sin(coarse.astype(jnp.float32) * angle)[:, None, :]
    cos_f = jnp.cos(fine.astype(jnp.float32) * angle)[None, :, :]
    sin_f = jnp.sin(fine.astype(jnp.float32) * angle)[None, :, :]
    rows = coarse_count * fine_count
    cos_t = (cos_c * cos_f - sin_c * sin_f).reshape(rows, length)[:length]
    sin_t = (sin_c * cos_f + cos_c * sin_f).reshape(rows, length)[:length]
    factor = 1.0 / math.sqrt(length)
    return (cos_t * factor).astype(jnp.bfloat16), (sin_t * factor).astype(jnp.bfloat16)


def complex_table(length):
    cos_t, sin_t = dft_tables(length)
    top = jnp.concatenate([cos_t, -sin_t], axis=1)
    bottom = jnp.concatenate([sin_t, cos_t], axis=1)
    return jnp.concatenate([top, bottom], axis=0)


def route_fibres(spectra, kernel, owner, offset, sky_count):
    fibre_count = spectra.shape[0]
    capacity = fibre_count * 5 // (4 * sky_count)
    block = 2 * capacity
    slots_all = sky_count * block
    target = owner[:, 0]
    order = jnp.arange(fibre_count, dtype=jnp.int32)
    same = (target[:, None] == target[None, :]) & (order[None, :] < order[:, None])
    before = jnp.sum(same.astype(jnp.int32), axis=1)
    first_slot = target * block + before
    second_slot = ((target + 1) % sky_count) * block + capacity + before
    slot_ids = jnp.arange(slots_all, dtype=jnp.int32)
    pick = (
        (slot_ids[:, None] == first_slot[None, :]) | (slot_ids[:, None] == second_slot[None, :])
    ).astype(jnp.bfloat16)
    row = (offset // NY).astype(jnp.bfloat16)[:, None]
    col = (offset % NY).astype(jnp.bfloat16)[:, None]
    packed = jnp.concatenate([spectra, kernel, row, col], axis=1)
    send = jnp.dot(pick, packed, preferred_element_type=jnp.float32).astype(jnp.bfloat16)
    send = send.reshape(sky_count, block * packed.shape[1])
    got = lax.all_to_all(send, "sky", split_axis=0, concat_axis=0, tiled=True)
    return got.reshape(slots_all, packed.shape[1]), capacity, block


def grid_tile(got, slab_width, taps, tile_rows, capacity, block):
    slots_all = got.shape[0]
    values = got[:, :slab_width]
    weights = got[:, slab_width : slab_width + taps].astype(jnp.float32)
    slot_ids = jnp.arange(slots_all, dtype=jnp.int32)
    shift = jnp.where(slot_ids % block >= capacity, tile_rows, 0)
    corner_row = got[:, slab_width + taps].astype(jnp.int32) - shift
    corner_col = got[:, slab_width + taps + 1].astype(jnp.int32)
    rows = jnp.arange(tile_rows, dtype=jnp.int32)
    columns = jnp.arange(NY, dtype=jnp.int32)
    spread = jnp.zeros((slots_all, tile_rows, NY), jnp.float32)
    for step_a in range(KSIDE):
        active = rows[None, :] == (corner_row + step_a)[:, None]
        line = jnp.zeros((slots_all, NY), jnp.float32)
        for step_b in range(KSIDE):
            placed = columns[None, :] == ((corner_col + step_b) % NY)[:, None]
            line = line + jnp.where(placed, weights[:, step_a * KSIDE + step_b][:, None], 0.0)
        spread = spread + jnp.where(active[:, :, None], line[:, None, :], 0.0)
    spread_bf = spread.astype(jnp.bfloat16).reshape(slots_all, tile_rows * NY)
    cube_t = lax.dot_general(
        values, spread_bf, (((0,), (0,)), ((), ())), preferred_element_type=jnp.float32
    )
    return cube_t.astype(jnp.bfloat16)


def shards(spectra, kernel, owner, offset):
    sky_count = lax.axis_size("sky")
    gz_count = lax.axis_size("gz")
    devices = sky_count * gz_count
    slab_width = spectra.shape[1]
    taps = kernel.shape[1]
    tile_rows = NX // sky_count
    per_dev = NY // devices

    got, capacity, block = route_fibres(spectra, kernel, owner, offset, sky_count)
    cube_t = grid_tile(got, slab_width, taps, tile_rows, capacity, block)
    cube_w = lax.all_to_all(cube_t, "gz", split_axis=1, concat_axis=0, tiled=True)
    rows_dev = tile_rows // gz_count
    cube_w = cube_w.reshape(NW, rows_dev, NY)

    cos_y, sin_y = dft_tables(NY)
    table_y = lax.optimization_barrier(jnp.concatenate([cos_y, -sin_y], axis=1))
    cos_w, sin_w = lax.optimization_barrier(twiddles(NW))
    table_x = complex_table(NX).reshape(2, devices, rows_dev, 2, NX)
    table_x = lax.optimization_barrier(table_x)

    first = jnp.einsum(
        "wxy,yrk->kxrw", cube_w, table_y.reshape(NY, 2, NY), preferred_element_type=jnp.float32
    ).astype(jnp.bfloat16)
    swapped = jnp.stack([first[:, :, 1], -first[:, :, 0]], axis=2)
    first_t = first.reshape(NY * rows_dev * 2, NW)
    swapped = swapped.reshape(NY * rows_dev * 2, NW)
    second = jnp.dot(first_t, cos_w, preferred_element_type=jnp.float32) + jnp.dot(
        swapped, sin_w, preferred_element_type=jnp.float32
    )
    second = second.astype(jnp.bfloat16).reshape(devices, per_dev * rows_dev * 2, NW)
    pencils = lax.all_to_all(second, ("sky", "gz"), split_axis=0, concat_axis=0, tiled=True)
    pencils = pencils.reshape(devices, per_dev, rows_dev, 2, NW)
    return jnp.einsum("sqxRv,RsxUu->Uuqv", pencils, table_x, preferred_element_type=jnp.float32)


def solution(mesh):
    in_specs = (P("sky", "gz"), P("sky", None), P("sky", None), P("sky"))
    out_specs = P(None, None, ("sky", "gz"), None)
    return jax.shard_map(shards, mesh=mesh, in_specs=in_specs, out_specs=out_specs, check_vma=False)
```

```python
import math

import jax
import jax.numpy as jnp
from jax import lax
from jax.sharding import PartitionSpec as P

NX = 256
NY = 256
NW = 1032
KSIDE = 4


def dft_tables(length):
    steps = jnp.arange(length, dtype=jnp.int32)
    phase = steps[:, None] * steps[None, :] % length
    angles = phase.astype(jnp.float32) * (2.0 * math.pi / length)
    factor = 1.0 / math.sqrt(length)
    return (
        (jnp.cos(angles) * factor).astype(jnp.bfloat16),
        (jnp.sin(angles) * factor).astype(jnp.bfloat16),
    )


def twiddles(length, fine_count=16):
    coarse_count = -(-length // fine_count)
    steps = jnp.arange(length, dtype=jnp.int32)
    angle = 2.0 * math.pi / length
    coarse = (jnp.arange(coarse_count, dtype=jnp.int32)[:, None] * fine_count * steps[None, :]) % length
    fine = (jnp.arange(fine_count, dtype=jnp.int32)[:, None] * steps[None, :]) % length
    cos_c = jnp.cos(coarse.astype(jnp.float32) * angle)[:, None, :]
    sin_c = jnp.sin(coarse.astype(jnp.float32) * angle)[:, None, :]
    cos_f = jnp.cos(fine.astype(jnp.float32) * angle)[None, :, :]
    sin_f = jnp.sin(fine.astype(jnp.float32) * angle)[None, :, :]
    rows = coarse_count * fine_count
    cos_t = (cos_c * cos_f - sin_c * sin_f).reshape(rows, length)[:length]
    sin_t = (sin_c * cos_f + cos_c * sin_f).reshape(rows, length)[:length]
    factor = 1.0 / math.sqrt(length)
    return (cos_t * factor).astype(jnp.bfloat16), (sin_t * factor).astype(jnp.bfloat16)


def complex_table(length):
    cos_t, sin_t = dft_tables(length)
    top = jnp.concatenate([cos_t, -sin_t], axis=1)
    bottom = jnp.concatenate([sin_t, cos_t], axis=1)
    return jnp.concatenate([top, bottom], axis=0)


def route_fibres(spectra, kernel, owner, offset, sky_count):
    fibre_count = spectra.shape[0]
    capacity = fibre_count * 5 // (4 * sky_count)
    block = 2 * capacity
    slots_all = sky_count * block
    target = owner[:, 0]
    order = jnp.arange(fibre_count, dtype=jnp.int32)
    same = (target[:, None] == target[None, :]) & (order[None, :] < order[:, None])
    before = jnp.sum(same.astype(jnp.int32), axis=1)
    first_slot = target * block + before
    second_slot = ((target + 1) % sky_count) * block + capacity + before
    slot_ids = jnp.arange(slots_all, dtype=jnp.int32)
    pick = (
        (slot_ids[:, None] == first_slot[None, :]) | (slot_ids[:, None] == second_slot[None, :])
    ).astype(jnp.bfloat16)
    row = (offset // NY).astype(jnp.bfloat16)[:, None]
    col = (offset % NY).astype(jnp.bfloat16)[:, None]
    packed = jnp.concatenate([spectra, kernel, row, col], axis=1)
    send = jnp.dot(pick, packed, preferred_element_type=jnp.float32).astype(jnp.bfloat16)
    send = send.reshape(sky_count, block * packed.shape[1])
    got = lax.all_to_all(send, "sky", split_axis=0, concat_axis=0, tiled=True)
    return got.reshape(slots_all, packed.shape[1]), capacity, block


def grid_tile(got, slab_width, taps, tile_rows, capacity, block):
    slots_all = got.shape[0]
    values = got[:, :slab_width]
    weights = got[:, slab_width : slab_width + taps].astype(jnp.float32)
    slot_ids = jnp.arange(slots_all, dtype=jnp.int32)
    shift = jnp.where(slot_ids % block >= capacity, tile_rows, 0)
    corner_row = got[:, slab_width + taps].astype(jnp.int32) - shift
    corner_col = got[:, slab_width + taps + 1].astype(jnp.int32)
    rows = jnp.arange(tile_rows, dtype=jnp.int32)
    columns = jnp.arange(NY, dtype=jnp.int32)
    spread = jnp.zeros((slots_all, tile_rows, NY), jnp.float32)
    for step_a in range(KSIDE):
        active = rows[None, :] == (corner_row + step_a)[:, None]
        line = jnp.zeros((slots_all, NY), jnp.float32)
        for step_b in range(KSIDE):
            placed = columns[None, :] == ((corner_col + step_b) % NY)[:, None]
            line = line + jnp.where(placed, weights[:, step_a * KSIDE + step_b][:, None], 0.0)
        spread = spread + jnp.where(active[:, :, None], line[:, None, :], 0.0)
    spread_bf = spread.astype(jnp.bfloat16).reshape(slots_all, tile_rows * NY)
    cube_t = lax.dot_general(
        values, spread_bf, (((0,), (0,)), ((), ())), preferred_element_type=jnp.float32
    )
    return cube_t.astype(jnp.bfloat16)


def shards(spectra, kernel, owner, offset):
    sky_count = lax.axis_size("sky")
    gz_count = lax.axis_size("gz")
    devices = sky_count * gz_count
    slab_width = spectra.shape[1]
    taps = kernel.shape[1]
    tile_rows = NX // sky_count
    per_dev = NY // devices

    got, capacity, block = route_fibres(spectra, kernel, owner, offset, sky_count)
    cube_t = grid_tile(got, slab_width, taps, tile_rows, capacity, block)
    cube_w = lax.all_to_all(cube_t, "gz", split_axis=1, concat_axis=0, tiled=True)
    rows_dev = tile_rows // gz_count
    cube_w = cube_w.reshape(NW, rows_dev, NY)

    cos_y, sin_y = dft_tables(NY)
    table_y = jnp.concatenate([cos_y, -sin_y], axis=1)
    padded_nw = -(-NW // 128) * 128
    edge = ((0, padded_nw - NW), (0, padded_nw - NW))
    cos_w, sin_w = [jnp.pad(t, edge) for t in twiddles(NW)]
    table_x = complex_table(NX).reshape(2, devices, rows_dev, 2, NX)
    table_y, cos_w, sin_w, table_x = lax.optimization_barrier((table_y, cos_w, sin_w, table_x))

    cube_yw = jnp.pad(jnp.transpose(cube_w, (2, 1, 0)), ((0, 0), (0, 0), (0, padded_nw - NW)))
    first = jnp.einsum("yxw,yK->xKw", cube_yw, table_y, preferred_element_type=jnp.float32)
    first = first.astype(jnp.bfloat16).reshape(2 * NY * rows_dev, padded_nw)
    by_cos = jnp.dot(first, cos_w, preferred_element_type=jnp.float32)
    by_sin = jnp.dot(first, sin_w, preferred_element_type=jnp.float32)
    by_cos = by_cos.reshape(rows_dev, 2, NY, padded_nw)
    by_sin = by_sin.reshape(rows_dev, 2, NY, padded_nw)
    second = jnp.stack([by_cos[:, 0] + by_sin[:, 1], by_cos[:, 1] - by_sin[:, 0]], axis=2)
    second = jnp.transpose(second, (1, 0, 2, 3))
    second = second.astype(jnp.bfloat16).reshape(devices, per_dev * rows_dev * 2, padded_nw)
    pencils = lax.all_to_all(second, ("sky", "gz"), split_axis=0, concat_axis=0, tiled=True)
    pencils = pencils.reshape(devices, per_dev, rows_dev, 2, padded_nw)[..., :NW]
    return jnp.einsum("sqxRv,RsxUu->Uuqv", pencils, table_x, preferred_element_type=jnp.float32)


def solution(mesh):
    in_specs = (P("sky", "gz"), P("sky", None), P("sky", None), P("sky"))
    out_specs = P(None, None, ("sky", "gz"), None)
    return jax.shard_map(shards, mesh=mesh, in_specs=in_specs, out_specs=out_specs, check_vma=False)
```

```python
import math

import jax
import jax.numpy as jnp
from jax import lax
from jax.sharding import PartitionSpec as P

NX = 256
NY = 256
NW = 1032
KSIDE = 4


def dft_tables(length):
    steps = jnp.arange(length, dtype=jnp.int32)
    phase = steps[:, None] * steps[None, :] % length
    angles = phase.astype(jnp.float32) * (2.0 * math.pi / length)
    factor = 1.0 / math.sqrt(length)
    return (
        (jnp.cos(angles) * factor).astype(jnp.bfloat16),
        (jnp.sin(angles) * factor).astype(jnp.bfloat16),
    )


def twiddles(length, fine_count=16):
    coarse_count = -(-length // fine_count)
    steps = jnp.arange(length, dtype=jnp.int32)
    angle = 2.0 * math.pi / length
    coarse = (jnp.arange(coarse_count, dtype=jnp.int32)[:, None] * fine_count * steps[None, :]) % length
    fine = (jnp.arange(fine_count, dtype=jnp.int32)[:, None] * steps[None, :]) % length
    cos_c = jnp.cos(coarse.astype(jnp.float32) * angle)[:, None, :]
    sin_c = jnp.sin(coarse.astype(jnp.float32) * angle)[:, None, :]
    cos_f = jnp.cos(fine.astype(jnp.float32) * angle)[None, :, :]
    sin_f = jnp.sin(fine.astype(jnp.float32) * angle)[None, :, :]
    rows = coarse_count * fine_count
    cos_t = (cos_c * cos_f - sin_c * sin_f).reshape(rows, length)[:length]
    sin_t = (sin_c * cos_f + cos_c * sin_f).reshape(rows, length)[:length]
    factor = 1.0 / math.sqrt(length)
    return (cos_t * factor).astype(jnp.bfloat16), (sin_t * factor).astype(jnp.bfloat16)


def complex_table(length):
    cos_t, sin_t = dft_tables(length)
    top = jnp.concatenate([cos_t, -sin_t], axis=1)
    bottom = jnp.concatenate([sin_t, cos_t], axis=1)
    return jnp.concatenate([top, bottom], axis=0)


def route_fibres(spectra, kernel, owner, offset, sky_count):
    fibre_count = spectra.shape[0]
    capacity = fibre_count * 5 // (4 * sky_count)
    block = 2 * capacity
    slots_all = sky_count * block
    target = owner[:, 0]
    order = jnp.arange(fibre_count, dtype=jnp.int32)
    same = (target[:, None] == target[None, :]) & (order[None, :] < order[:, None])
    before = jnp.sum(same.astype(jnp.int32), axis=1)
    first_slot = target * block + before
    second_slot = ((target + 1) % sky_count) * block + capacity + before
    slot_ids = jnp.arange(slots_all, dtype=jnp.int32)
    pick = (
        (slot_ids[:, None] == first_slot[None, :]) | (slot_ids[:, None] == second_slot[None, :])
    ).astype(jnp.bfloat16)
    row = (offset // NY).astype(jnp.bfloat16)[:, None]
    col = (offset % NY).astype(jnp.bfloat16)[:, None]
    packed = jnp.concatenate([spectra, kernel, row, col], axis=1)
    send = jnp.dot(pick, packed, preferred_element_type=jnp.float32).astype(jnp.bfloat16)
    send = send.reshape(sky_count, block, packed.shape[1])
    got = lax.all_to_all(send, "sky", split_axis=0, concat_axis=0, tiled=True)
    return got.reshape(slots_all, packed.shape[1]), capacity, block


def grid_tile(got, slab_width, taps, tile_rows, capacity, block):
    slots_all = got.shape[0]
    values = got[:, :slab_width]
    slot_ids = jnp.arange(slots_all, dtype=jnp.int32)
    shift = jnp.where(slot_ids % block >= capacity, tile_rows, 0)
    corner_row = got[:, slab_width + taps].astype(jnp.int32) - shift
    corner_col = got[:, slab_width + taps + 1].astype(jnp.int32)
    cells = jnp.arange(tile_rows * NY, dtype=jnp.int32)
    cell_row = cells // NY
    cell_col = cells % NY
    lag = cell_row[None, :] - corner_row[:, None]
    shift = (cell_col[None, :] - corner_col[:, None]) % NY
    spread_bf = jnp.zeros((slots_all, tile_rows * NY), jnp.bfloat16)
    for step_a in range(KSIDE):
        for step_b in range(KSIDE):
            hit = (lag == step_a) & (shift == step_b)
            tap = got[:, slab_width + step_a * KSIDE + step_b][:, None]
            spread_bf = jnp.where(hit, tap, spread_bf)
    cube_t = lax.dot_general(
        values, spread_bf, (((0,), (0,)), ((), ())), preferred_element_type=jnp.float32
    )
    return cube_t.astype(jnp.bfloat16)


def shards(spectra, kernel, owner, offset):
    sky_count = lax.axis_size("sky")
    gz_count = lax.axis_size("gz")
    devices = sky_count * gz_count
    slab_width = spectra.shape[1]
    taps = kernel.shape[1]
    tile_rows = NX // sky_count
    per_dev = NY // devices

    got, capacity, block = route_fibres(spectra, kernel, owner, offset, sky_count)
    cube_t = grid_tile(got, slab_width, taps, tile_rows, capacity, block)
    cube_w = lax.all_to_all(cube_t, "gz", split_axis=1, concat_axis=0, tiled=True)
    rows_dev = tile_rows // gz_count
    cube_w = cube_w.reshape(NW, rows_dev, NY)

    cos_y, sin_y = dft_tables(NY)
    table_y = jnp.concatenate([cos_y, -sin_y], axis=1)
    padded_nw = -(-NW // 128) * 128
    edge = ((0, padded_nw - NW), (0, padded_nw - NW))
    cos_w, sin_w = [jnp.pad(t, edge) for t in twiddles(NW)]
    table_x = complex_table(NX).reshape(2, devices, rows_dev, 2, NX)
    table_y, cos_w, sin_w, table_x = lax.optimization_barrier((table_y, cos_w, sin_w, table_x))

    cube_yw = jnp.pad(jnp.transpose(cube_w, (2, 1, 0)), ((0, 0), (0, 0), (0, padded_nw - NW)))
    first = jnp.einsum("yxw,yK->xKw", cube_yw, table_y, preferred_element_type=jnp.float32)
    first = first.astype(jnp.bfloat16).reshape(2 * NY * rows_dev, padded_nw)
    by_cos = jnp.dot(first, cos_w, preferred_element_type=jnp.float32)
    by_sin = jnp.dot(first, sin_w, preferred_element_type=jnp.float32)
    by_cos = by_cos.reshape(rows_dev, 2, NY, padded_nw)
    by_sin = by_sin.reshape(rows_dev, 2, NY, padded_nw)
    second = jnp.stack([by_cos[:, 0] + by_sin[:, 1], by_cos[:, 1] - by_sin[:, 0]], axis=2)
    second = jnp.transpose(second, (1, 0, 2, 3))
    second = second.astype(jnp.bfloat16).reshape(devices, per_dev * rows_dev * 2, padded_nw)
    pencils = lax.all_to_all(second, ("sky", "gz"), split_axis=0, concat_axis=0, tiled=True)
    pencils = pencils.reshape(devices, per_dev, rows_dev, 2, padded_nw)[..., :NW]
    return jnp.einsum("sqxRv,RsxUu->Uuqv", pencils, table_x, preferred_element_type=jnp.float32)


def solution(mesh):
    in_specs = (P("sky", "gz"), P("sky", None), P("sky", None), P("sky"))
    out_specs = P(None, None, ("sky", "gz"), None)
    return jax.shard_map(shards, mesh=mesh, in_specs=in_specs, out_specs=out_specs, check_vma=False)
```

```python
import math

import jax
import jax.numpy as jnp
from jax import lax
from jax.sharding import PartitionSpec as P

NX = 256
NY = 256
NW = 1032
KSIDE = 4


def dft_tables(length):
    steps = jnp.arange(length, dtype=jnp.int32)
    phase = steps[:, None] * steps[None, :] % length
    angles = phase.astype(jnp.float32) * (2.0 * math.pi / length)
    factor = 1.0 / math.sqrt(length)
    return (
        (jnp.cos(angles) * factor).astype(jnp.bfloat16),
        (jnp.sin(angles) * factor).astype(jnp.bfloat16),
    )


def twiddles(length, fine_count=16):
    coarse_count = -(-length // fine_count)
    steps = jnp.arange(length, dtype=jnp.int32)
    angle = 2.0 * math.pi / length
    coarse = (jnp.arange(coarse_count, dtype=jnp.int32)[:, None] * fine_count * steps[None, :]) % length
    fine = (jnp.arange(fine_count, dtype=jnp.int32)[:, None] * steps[None, :]) % length
    cos_c = jnp.cos(coarse.astype(jnp.float32) * angle)[:, None, :]
    sin_c = jnp.sin(coarse.astype(jnp.float32) * angle)[:, None, :]
    cos_f = jnp.cos(fine.astype(jnp.float32) * angle)[None, :, :]
    sin_f = jnp.sin(fine.astype(jnp.float32) * angle)[None, :, :]
    rows = coarse_count * fine_count
    cos_t = (cos_c * cos_f - sin_c * sin_f).reshape(rows, length)[:length]
    sin_t = (sin_c * cos_f + cos_c * sin_f).reshape(rows, length)[:length]
    factor = 1.0 / math.sqrt(length)
    return (cos_t * factor).astype(jnp.bfloat16), (sin_t * factor).astype(jnp.bfloat16)


def complex_table(length):
    cos_t, sin_t = dft_tables(length)
    top = jnp.concatenate([cos_t, -sin_t], axis=1)
    bottom = jnp.concatenate([sin_t, cos_t], axis=1)
    return jnp.concatenate([top, bottom], axis=0)


def route_fibres(spectra, kernel, owner, offset, sky_count):
    fibre_count = spectra.shape[0]
    capacity = fibre_count * 5 // (4 * sky_count)
    block = 2 * capacity
    slots_all = sky_count * block
    target = owner[:, 0]
    order = jnp.arange(fibre_count, dtype=jnp.int32)
    same = (target[:, None] == target[None, :]) & (order[None, :] < order[:, None])
    before = jnp.sum(same.astype(jnp.int32), axis=1)
    first_slot = target * block + before
    second_slot = ((target + 1) % sky_count) * block + capacity + before
    slot_ids = jnp.arange(slots_all, dtype=jnp.int32)
    pick = (
        (slot_ids[:, None] == first_slot[None, :]) | (slot_ids[:, None] == second_slot[None, :])
    ).astype(jnp.bfloat16)
    row = (offset // NY).astype(jnp.bfloat16)[:, None]
    col = (offset % NY).astype(jnp.bfloat16)[:, None]
    packed = jnp.concatenate([spectra, kernel, row, col], axis=1)
    send = jnp.dot(pick, packed, preferred_element_type=jnp.float32).astype(jnp.bfloat16)
    send = send.reshape(sky_count, block, packed.shape[1])
    got = lax.all_to_all(send, "sky", split_axis=0, concat_axis=0, tiled=True)
    return got.reshape(slots_all, packed.shape[1]), capacity, block


def grid_tile(got, slab_width, taps, tile_rows, capacity, block):
    slots_all = got.shape[0]
    values = got[:, :slab_width]
    slot_ids = jnp.arange(slots_all, dtype=jnp.int32)
    shift = jnp.where(slot_ids % block >= capacity, tile_rows, 0)
    corner_row = got[:, slab_width + taps].astype(jnp.int32) - shift
    corner_col = got[:, slab_width + taps + 1].astype(jnp.int32)
    rows = jnp.arange(tile_rows, dtype=jnp.int32)
    columns = jnp.arange(NY, dtype=jnp.int32)
    spread = jnp.zeros((tile_rows, slots_all, NY), jnp.bfloat16)
    for step_a in range(KSIDE):
        line = jnp.zeros((slots_all, NY), jnp.bfloat16)
        for step_b in range(KSIDE):
            placed = columns[None, :] == ((corner_col + step_b) % NY)[:, None]
            line = jnp.where(placed, got[:, slab_width + step_a * KSIDE + step_b][:, None], line)
        active = rows[:, None] == (corner_row + step_a)[None, :]
        spread = jnp.where(active[:, :, None], line[None, :, :], spread)
    cube_t = jnp.einsum("sw,xsc->wxc", values, spread, preferred_element_type=jnp.float32)
    cube_t = cube_t.reshape(slab_width, tile_rows * NY)
    return cube_t.astype(jnp.bfloat16)


def shards(spectra, kernel, owner, offset):
    sky_count = lax.axis_size("sky")
    gz_count = lax.axis_size("gz")
    devices = sky_count * gz_count
    slab_width = spectra.shape[1]
    taps = kernel.shape[1]
    tile_rows = NX // sky_count
    per_dev = NY // devices

    got, capacity, block = route_fibres(spectra, kernel, owner, offset, sky_count)
    cube_t = grid_tile(got, slab_width, taps, tile_rows, capacity, block)
    cube_w = lax.all_to_all(cube_t, "gz", split_axis=1, concat_axis=0, tiled=True)
    rows_dev = tile_rows // gz_count
    cube_w = cube_w.reshape(NW, rows_dev, NY)

    cos_y, sin_y = dft_tables(NY)
    table_y = jnp.concatenate([cos_y, -sin_y], axis=1)
    padded_nw = -(-NW // 128) * 128
    edge = ((0, padded_nw - NW), (0, padded_nw - NW))
    cos_w, sin_w = [jnp.pad(t, edge) for t in twiddles(NW)]
    table_x = complex_table(NX).reshape(2, devices, rows_dev, 2, NX)
    table_y, cos_w, sin_w, table_x = lax.optimization_barrier((table_y, cos_w, sin_w, table_x))

    cube_yw = jnp.pad(jnp.transpose(cube_w, (2, 1, 0)), ((0, 0), (0, 0), (0, padded_nw - NW)))
    first = jnp.einsum("yxw,yK->xKw", cube_yw, table_y, preferred_element_type=jnp.float32)
    first = first.astype(jnp.bfloat16).reshape(2 * NY * rows_dev, padded_nw)
    by_cos = jnp.dot(first, cos_w, preferred_element_type=jnp.float32)
    by_sin = jnp.dot(first, sin_w, preferred_element_type=jnp.float32)
    by_cos = by_cos.reshape(rows_dev, 2, NY, padded_nw)
    by_sin = by_sin.reshape(rows_dev, 2, NY, padded_nw)
    second = jnp.stack([by_cos[:, 0] + by_sin[:, 1], by_cos[:, 1] - by_sin[:, 0]], axis=2)
    second = jnp.transpose(second, (1, 0, 2, 3))
    second = second.astype(jnp.bfloat16).reshape(devices, per_dev * rows_dev * 2, padded_nw)
    pencils = lax.all_to_all(second, ("sky", "gz"), split_axis=0, concat_axis=0, tiled=True)
    pencils = pencils.reshape(devices, per_dev, rows_dev, 2, padded_nw)[..., :NW]
    return jnp.einsum("sqxRv,RsxUu->Uuqv", pencils, table_x, preferred_element_type=jnp.float32)


def solution(mesh):
    in_specs = (P("sky", "gz"), P("sky", None), P("sky", None), P("sky"))
    out_specs = P(None, None, ("sky", "gz"), None)
    return jax.shard_map(shards, mesh=mesh, in_specs=in_specs, out_specs=out_specs, check_vma=False)
```

```python
import math

import jax
import jax.numpy as jnp
from jax import lax
from jax.sharding import PartitionSpec as P

NX = 256
NY = 256
NW = 1032
KSIDE = 4


def dft_tables(length, steps=None):
    if steps is None:
        steps = jnp.arange(length, dtype=jnp.int32)
    phase = steps[:, None] * steps[None, :] % length
    angles = phase.astype(jnp.float32) * (2.0 * math.pi / length)
    factor = 1.0 / math.sqrt(length)
    return (
        (jnp.cos(angles) * factor).astype(jnp.bfloat16),
        (jnp.sin(angles) * factor).astype(jnp.bfloat16),
    )


def twiddles(steps, fine_count=16):
    length = steps.shape[0]
    coarse_count = -(-length // fine_count)
    angle = 2.0 * math.pi / length
    coarse = (jnp.arange(coarse_count, dtype=jnp.int32)[:, None] * fine_count * steps[None, :]) % length
    fine = (jnp.arange(fine_count, dtype=jnp.int32)[:, None] * steps[None, :]) % length
    cos_c = jnp.cos(coarse.astype(jnp.float32) * angle)[:, None, :]
    sin_c = jnp.sin(coarse.astype(jnp.float32) * angle)[:, None, :]
    cos_f = jnp.cos(fine.astype(jnp.float32) * angle)[None, :, :]
    sin_f = jnp.sin(fine.astype(jnp.float32) * angle)[None, :, :]
    rows = coarse_count * fine_count
    cos_t = (cos_c * cos_f - sin_c * sin_f).reshape(rows, length)[:length]
    sin_t = (sin_c * cos_f + cos_c * sin_f).reshape(rows, length)[:length]
    factor = 1.0 / math.sqrt(length)
    return (cos_t * factor).astype(jnp.bfloat16), (sin_t * factor).astype(jnp.bfloat16)


def complex_table(length, steps=None):
    cos_t, sin_t = dft_tables(length, steps)
    top = jnp.concatenate([cos_t, -sin_t], axis=1)
    bottom = jnp.concatenate([sin_t, cos_t], axis=1)
    return jnp.concatenate([top, bottom], axis=0)


def route_fibres(spectra, kernel, owner, offset, sky_count):
    fibre_count = spectra.shape[0]
    capacity = fibre_count * 5 // (4 * sky_count)
    block = 2 * capacity
    slots_all = sky_count * block
    target = owner[:, 0]
    order = jnp.arange(fibre_count, dtype=jnp.int32)
    same = (target[:, None] == target[None, :]) & (order[None, :] < order[:, None])
    before = jnp.sum(same.astype(jnp.int32), axis=1)
    first_slot = target * block + before
    second_slot = ((target + 1) % sky_count) * block + capacity + before
    slot_ids = jnp.arange(slots_all, dtype=jnp.int32)
    pick = (
        (slot_ids[:, None] == first_slot[None, :]) | (slot_ids[:, None] == second_slot[None, :])
    ).astype(jnp.bfloat16)
    row = (offset // NY).astype(jnp.bfloat16)[:, None]
    col = (offset % NY).astype(jnp.bfloat16)[:, None]
    packed = jnp.concatenate([spectra, kernel, row, col], axis=1)
    send = jnp.dot(pick, packed, preferred_element_type=jnp.float32).astype(jnp.bfloat16)
    send = send.reshape(sky_count, block, packed.shape[1])
    got = lax.all_to_all(send, "sky", split_axis=0, concat_axis=0, tiled=True)
    return got.reshape(slots_all, packed.shape[1]), capacity, block


def grid_tile(got, slab_width, taps, tile_rows, capacity, block):
    slots_all = got.shape[0]
    values = got[:, :slab_width]
    slot_ids = jnp.arange(slots_all, dtype=jnp.int32)
    shift = jnp.where(slot_ids % block >= capacity, tile_rows, 0)
    corner_row = got[:, slab_width + taps].astype(jnp.int32) - shift
    corner_col = got[:, slab_width + taps + 1].astype(jnp.int32)
    rows = jnp.arange(tile_rows, dtype=jnp.int32)
    columns = jnp.arange(NY, dtype=jnp.int32)
    spread = jnp.zeros((tile_rows, slots_all, NY), jnp.bfloat16)
    for step_a in range(KSIDE):
        line = jnp.zeros((slots_all, NY), jnp.bfloat16)
        for step_b in range(KSIDE):
            placed = columns[None, :] == ((corner_col + step_b) % NY)[:, None]
            line = jnp.where(placed, got[:, slab_width + step_a * KSIDE + step_b][:, None], line)
        active = rows[:, None] == (corner_row + step_a)[None, :]
        spread = jnp.where(active[:, :, None], line[None, :, :], spread)
    cube_t = jnp.einsum("sw,xsc->wxc", values, spread, preferred_element_type=jnp.float32)
    cube_t = cube_t.reshape(slab_width, tile_rows * NY)
    return cube_t.astype(jnp.bfloat16)


def shards(spectra, kernel, owner, offset):
    sky_count = lax.axis_size("sky")
    gz_count = lax.axis_size("gz")
    devices = sky_count * gz_count
    slab_width = spectra.shape[1]
    taps = kernel.shape[1]
    tile_rows = NX // sky_count
    per_dev = NY // devices

    got, capacity, block = route_fibres(spectra, kernel, owner, offset, sky_count)
    cube_t = grid_tile(got, slab_width, taps, tile_rows, capacity, block)
    steps_w = jnp.arange(NW, dtype=jnp.int32)
    steps_y = jnp.arange(NY, dtype=jnp.int32)
    steps_x = jnp.arange(NX, dtype=jnp.int32)
    cube_t, steps_w, steps_y, steps_x = lax.optimization_barrier((cube_t, steps_w, steps_y, steps_x))
    cube_w = lax.all_to_all(cube_t, "gz", split_axis=1, concat_axis=0, tiled=True)
    rows_dev = tile_rows // gz_count
    cube_w = cube_w.reshape(NW, rows_dev, NY)

    cos_y, sin_y = dft_tables(NY, steps_y)
    table_y = jnp.concatenate([cos_y, -sin_y], axis=1)
    padded_nw = -(-NW // 128) * 128
    edge = ((0, padded_nw - NW), (0, padded_nw - NW))
    cos_w, sin_w = [jnp.pad(t, edge) for t in twiddles(steps_w)]
    table_x = complex_table(NX, steps_x).reshape(2, devices, rows_dev, 2, NX)
    table_y, cos_w, sin_w, table_x = lax.optimization_barrier((table_y, cos_w, sin_w, table_x))

    cube_yw = jnp.pad(jnp.transpose(cube_w, (2, 1, 0)), ((0, 0), (0, 0), (0, padded_nw - NW)))
    first = jnp.einsum("yxw,yK->xKw", cube_yw, table_y, preferred_element_type=jnp.float32)
    first = first.astype(jnp.bfloat16).reshape(2 * NY * rows_dev, padded_nw)
    by_cos = jnp.dot(first, cos_w, preferred_element_type=jnp.float32)
    by_sin = jnp.dot(first, sin_w, preferred_element_type=jnp.float32)
    by_cos = by_cos.reshape(rows_dev, 2, NY, padded_nw)
    by_sin = by_sin.reshape(rows_dev, 2, NY, padded_nw)
    second = jnp.stack([by_cos[:, 0] + by_sin[:, 1], by_cos[:, 1] - by_sin[:, 0]], axis=2)
    second = jnp.transpose(second, (1, 0, 2, 3))
    second = second.astype(jnp.bfloat16).reshape(devices, per_dev * rows_dev * 2, padded_nw)
    pencils = lax.all_to_all(second, ("sky", "gz"), split_axis=0, concat_axis=0, tiled=True)
    pencils = pencils.reshape(devices, per_dev, rows_dev, 2, padded_nw)[..., :NW]
    return jnp.einsum("sqxRv,RsxUu->Uuqv", pencils, table_x, preferred_element_type=jnp.float32)


def solution(mesh):
    in_specs = (P("sky", "gz"), P("sky", None), P("sky", None), P("sky"))
    out_specs = P(None, None, ("sky", "gz"), None)
    return jax.shard_map(shards, mesh=mesh, in_specs=in_specs, out_specs=out_specs, check_vma=False)
```

```python
import math

import jax
import jax.numpy as jnp
from jax import lax
from jax.sharding import PartitionSpec as P

NX = 256
NY = 256
NW = 1032
KSIDE = 4


def dft_tables(length, steps=None):
    if steps is None:
        steps = jnp.arange(length, dtype=jnp.int32)
    phase = steps[:, None] * steps[None, :] % length
    angles = phase.astype(jnp.float32) * (2.0 * math.pi / length)
    factor = 1.0 / math.sqrt(length)
    return (
        (jnp.cos(angles) * factor).astype(jnp.bfloat16),
        (jnp.sin(angles) * factor).astype(jnp.bfloat16),
    )


def twiddles(length, padded, fine_count=16):
    coarse_count = padded // fine_count
    steps = jnp.arange(padded, dtype=jnp.int32)
    angle = 2.0 * math.pi / length
    coarse = (jnp.arange(coarse_count, dtype=jnp.int32)[:, None] * fine_count * steps[None, :]) % length
    fine = (jnp.arange(fine_count, dtype=jnp.int32)[:, None] * steps[None, :]) % length
    cos_c = jnp.cos(coarse.astype(jnp.float32) * angle)[:, None, :]
    sin_c = jnp.sin(coarse.astype(jnp.float32) * angle)[:, None, :]
    cos_f = jnp.cos(fine.astype(jnp.float32) * angle)[None, :, :]
    sin_f = jnp.sin(fine.astype(jnp.float32) * angle)[None, :, :]
    cos_t = (cos_c * cos_f - sin_c * sin_f).reshape(padded, padded)
    sin_t = (sin_c * cos_f + cos_c * sin_f).reshape(padded, padded)
    inside = (steps[:, None] < length) & (steps[None, :] < length)
    factor = 1.0 / math.sqrt(length)
    cos_t = jnp.where(inside, cos_t * factor, 0.0).astype(jnp.bfloat16)
    sin_t = jnp.where(inside, sin_t * factor, 0.0).astype(jnp.bfloat16)
    return cos_t, sin_t


def complex_table(length, steps=None):
    cos_t, sin_t = dft_tables(length, steps)
    top = jnp.concatenate([cos_t, -sin_t], axis=1)
    bottom = jnp.concatenate([sin_t, cos_t], axis=1)
    return jnp.concatenate([top, bottom], axis=0)


def route_fibres(spectra, kernel, owner, offset, sky_count):
    fibre_count = spectra.shape[0]
    capacity = fibre_count * 5 // (4 * sky_count)
    block = 2 * capacity
    slots_all = sky_count * block
    target = owner[:, 0]
    order = jnp.arange(fibre_count, dtype=jnp.int32)
    same = (target[:, None] == target[None, :]) & (order[None, :] < order[:, None])
    before = jnp.sum(same.astype(jnp.int32), axis=1)
    first_slot = target * block + before
    second_slot = ((target + 1) % sky_count) * block + capacity + before
    slot_ids = jnp.arange(slots_all, dtype=jnp.int32)
    pick = (
        (slot_ids[:, None] == first_slot[None, :]) | (slot_ids[:, None] == second_slot[None, :])
    ).astype(jnp.bfloat16)
    row = (offset // NY).astype(jnp.bfloat16)[:, None]
    col = (offset % NY).astype(jnp.bfloat16)[:, None]
    packed = jnp.concatenate([spectra, kernel, row, col], axis=1)
    send = jnp.dot(pick, packed, preferred_element_type=jnp.float32).astype(jnp.bfloat16)
    send = send.reshape(sky_count, block, packed.shape[1])
    got = lax.all_to_all(send, "sky", split_axis=0, concat_axis=0, tiled=True)
    return got.reshape(slots_all, packed.shape[1]), capacity, block


def grid_tile(got, slab_width, taps, tile_rows, capacity, block):
    slots_all = got.shape[0]
    values = got[:, :slab_width]
    slot_ids = jnp.arange(slots_all, dtype=jnp.int32)
    shift = jnp.where(slot_ids % block >= capacity, tile_rows, 0)
    corner_row = got[:, slab_width + taps].astype(jnp.int32) - shift
    corner_col = got[:, slab_width + taps + 1].astype(jnp.int32)
    rows = jnp.arange(tile_rows, dtype=jnp.int32)
    columns = jnp.arange(NY, dtype=jnp.int32)
    spread = jnp.zeros((tile_rows, slots_all, NY), jnp.bfloat16)
    for step_a in range(KSIDE):
        line = jnp.zeros((slots_all, NY), jnp.bfloat16)
        for step_b in range(KSIDE):
            placed = columns[None, :] == ((corner_col + step_b) % NY)[:, None]
            line = jnp.where(placed, got[:, slab_width + step_a * KSIDE + step_b][:, None], line)
        active = rows[:, None] == (corner_row + step_a)[None, :]
        spread = jnp.where(active[:, :, None], line[None, :, :], spread)
    cube_t = jnp.einsum("sw,xsc->wxc", values, spread, preferred_element_type=jnp.float32)
    cube_t = cube_t.reshape(slab_width, tile_rows * NY)
    return cube_t.astype(jnp.bfloat16)


def shards(spectra, kernel, owner, offset):
    sky_count = lax.axis_size("sky")
    gz_count = lax.axis_size("gz")
    devices = sky_count * gz_count
    slab_width = spectra.shape[1]
    taps = kernel.shape[1]
    tile_rows = NX // sky_count
    per_dev = NY // devices

    got, capacity, block = route_fibres(spectra, kernel, owner, offset, sky_count)
    cube_t = grid_tile(got, slab_width, taps, tile_rows, capacity, block)
    steps_y = jnp.arange(NY, dtype=jnp.int32)
    steps_x = jnp.arange(NX, dtype=jnp.int32)
    cube_t, steps_y, steps_x = lax.optimization_barrier((cube_t, steps_y, steps_x))
    cube_w = lax.all_to_all(cube_t, "gz", split_axis=1, concat_axis=0, tiled=True)
    rows_dev = tile_rows // gz_count
    cube_w = cube_w.reshape(NW, rows_dev, NY)

    cos_y, sin_y = dft_tables(NY, steps_y)
    table_y = jnp.concatenate([cos_y, -sin_y], axis=1)
    padded_nw = -(-NW // 128) * 128
    cos_w, sin_w = twiddles(NW, padded_nw)
    table_x = complex_table(NX, steps_x).reshape(2, devices, rows_dev, 2, NX)
    table_y, cos_w, sin_w, table_x = lax.optimization_barrier((table_y, cos_w, sin_w, table_x))

    cube_yw = jnp.pad(jnp.transpose(cube_w, (2, 1, 0)), ((0, 0), (0, 0), (0, padded_nw - NW)))
    first = jnp.einsum("yxw,yK->xKw", cube_yw, table_y, preferred_element_type=jnp.float32)
    first = first.astype(jnp.bfloat16).reshape(2 * NY * rows_dev, padded_nw)
    by_cos = jnp.dot(first, cos_w, preferred_element_type=jnp.float32)
    by_sin = jnp.dot(first, sin_w, preferred_element_type=jnp.float32)
    by_cos = by_cos.reshape(rows_dev, 2, NY, padded_nw)
    by_sin = by_sin.reshape(rows_dev, 2, NY, padded_nw)
    second = jnp.stack([by_cos[:, 0] + by_sin[:, 1], by_cos[:, 1] - by_sin[:, 0]], axis=2)
    second = jnp.transpose(second, (1, 0, 2, 3))
    second = second.astype(jnp.bfloat16).reshape(devices, per_dev * rows_dev * 2, padded_nw)
    pencils = lax.all_to_all(second, ("sky", "gz"), split_axis=0, concat_axis=0, tiled=True)
    pencils = pencils.reshape(devices, per_dev, rows_dev, 2, padded_nw)[..., :NW]
    return jnp.einsum("sqxRv,RsxUu->Uuqv", pencils, table_x, preferred_element_type=jnp.float32)


def solution(mesh):
    in_specs = (P("sky", "gz"), P("sky", None), P("sky", None), P("sky"))
    out_specs = P(None, None, ("sky", "gz"), None)
    return jax.shard_map(shards, mesh=mesh, in_specs=in_specs, out_specs=out_specs, check_vma=False)
```

```python
import math

import jax
import jax.numpy as jnp
from jax import lax
from jax.sharding import PartitionSpec as P

NX = 256
NY = 256
NW = 1032
KSIDE = 4


def dft_tables(length, steps=None):
    if steps is None:
        steps = jnp.arange(length, dtype=jnp.int32)
    phase = steps[:, None] * steps[None, :] % length
    angles = phase.astype(jnp.float32) * (2.0 * math.pi / length)
    factor = 1.0 / math.sqrt(length)
    return (
        (jnp.cos(angles) * factor).astype(jnp.bfloat16),
        (jnp.sin(angles) * factor).astype(jnp.bfloat16),
    )


def twiddles(length, padded, fine_count=16):
    coarse_count = padded // fine_count
    steps = jnp.arange(padded, dtype=jnp.int32)
    angle = 2.0 * math.pi / length
    coarse = (jnp.arange(coarse_count, dtype=jnp.int32)[:, None] * fine_count * steps[None, :]) % length
    fine = (jnp.arange(fine_count, dtype=jnp.int32)[:, None] * steps[None, :]) % length
    cos_c = jnp.cos(coarse.astype(jnp.float32) * angle)[:, None, :]
    sin_c = jnp.sin(coarse.astype(jnp.float32) * angle)[:, None, :]
    cos_f = jnp.cos(fine.astype(jnp.float32) * angle)[None, :, :]
    sin_f = jnp.sin(fine.astype(jnp.float32) * angle)[None, :, :]
    cos_t = (cos_c * cos_f - sin_c * sin_f).reshape(padded, padded)
    sin_t = (sin_c * cos_f + cos_c * sin_f).reshape(padded, padded)
    inside = (steps[:, None] < length) & (steps[None, :] < length)
    factor = 1.0 / math.sqrt(length)
    cos_t = jnp.where(inside, cos_t * factor, 0.0).astype(jnp.bfloat16)
    sin_t = jnp.where(inside, sin_t * factor, 0.0).astype(jnp.bfloat16)
    return cos_t, sin_t


def complex_table(length, steps=None):
    cos_t, sin_t = dft_tables(length, steps)
    top = jnp.concatenate([cos_t, -sin_t], axis=1)
    bottom = jnp.concatenate([sin_t, cos_t], axis=1)
    return jnp.concatenate([top, bottom], axis=0)


def route_fibres(spectra, kernel, owner, offset, sky_count):
    fibre_count = spectra.shape[0]
    capacity = fibre_count * 5 // (4 * sky_count)
    block = 2 * capacity
    slots_all = sky_count * block
    target = owner[:, 0]
    order = jnp.arange(fibre_count, dtype=jnp.int32)
    same = (target[:, None] == target[None, :]) & (order[None, :] < order[:, None])
    before = jnp.sum(same.astype(jnp.int32), axis=1)
    first_slot = target * block + before
    second_slot = ((target + 1) % sky_count) * block + capacity + before
    slot_ids = jnp.arange(slots_all, dtype=jnp.int32)
    pick = (
        (slot_ids[:, None] == first_slot[None, :]) | (slot_ids[:, None] == second_slot[None, :])
    ).astype(jnp.bfloat16)
    row = (offset // NY).astype(jnp.bfloat16)[:, None]
    col = (offset % NY).astype(jnp.bfloat16)[:, None]
    packed = jnp.concatenate([spectra, kernel, row, col], axis=1)
    send = jnp.dot(pick, packed, preferred_element_type=jnp.float32).astype(jnp.bfloat16)
    send = send.reshape(sky_count, block, packed.shape[1])
    got = lax.all_to_all(send, "sky", split_axis=0, concat_axis=0, tiled=True)
    return got.reshape(slots_all, packed.shape[1]), capacity, block


def grid_rows(got, values, slab_width, row_ids, capacity, block):
    slots_all = got.shape[0]
    slot_ids = jnp.arange(slots_all, dtype=jnp.int32)
    shift = jnp.where(slot_ids % block >= capacity, NX // (slots_all // block), 0)
    corner_row = got[:, slab_width + KSIDE * KSIDE].astype(jnp.int32) - shift
    corner_col = got[:, slab_width + KSIDE * KSIDE + 1].astype(jnp.int32)
    columns = jnp.arange(NY, dtype=jnp.int32)
    spread = jnp.zeros((NY, row_ids.shape[0], slots_all), jnp.bfloat16)
    for step_a in range(KSIDE):
        line = jnp.zeros((NY, slots_all), jnp.bfloat16)
        for step_b in range(KSIDE):
            placed = columns[:, None] == ((corner_col + step_b) % NY)[None, :]
            tap = got[:, slab_width + step_a * KSIDE + step_b][None, :]
            line = jnp.where(placed, tap, line)
        active = row_ids[:, None] == (corner_row + step_a)[None, :]
        spread = jnp.where(active[None, :, :], line[:, None, :], spread)
    spread = spread.reshape(NY * row_ids.shape[0], slots_all)
    return jnp.dot(spread, values, preferred_element_type=jnp.float32).astype(jnp.bfloat16)


def shards(spectra, kernel, owner, offset):
    sky_count = lax.axis_size("sky")
    gz_count = lax.axis_size("gz")
    devices = sky_count * gz_count
    slab_width = spectra.shape[1]
    taps = kernel.shape[1]
    tile_rows = NX // sky_count
    per_dev = NY // devices

    got, capacity, block = route_fibres(spectra, kernel, owner, offset, sky_count)
    rows_dev = tile_rows // gz_count
    padded_nw = -(-NW // 128) * 128
    values = lax.all_gather(got[:, :slab_width], "gz", axis=1, tiled=True)
    values = jnp.pad(values, ((0, 0), (0, padded_nw - NW)))
    row_ids = lax.axis_index("gz") * rows_dev + jnp.arange(rows_dev, dtype=jnp.int32)
    cube_yw = grid_rows(got, values, slab_width, row_ids, capacity, block)
    cube_yw = cube_yw.reshape(NY, rows_dev, padded_nw)
    steps_y = jnp.arange(NY, dtype=jnp.int32)
    steps_x = jnp.arange(NX, dtype=jnp.int32)

    cos_y, sin_y = dft_tables(NY, steps_y)
    table_y = jnp.concatenate([cos_y, -sin_y], axis=1)
    cos_w, sin_w = twiddles(NW, padded_nw)
    table_x = complex_table(NX, steps_x).reshape(2, devices, rows_dev, 2, NX)
    table_y, cos_w, sin_w, table_x = lax.optimization_barrier((table_y, cos_w, sin_w, table_x))

    first = jnp.einsum("yxw,yK->xKw", cube_yw, table_y, preferred_element_type=jnp.float32)
    first = first.astype(jnp.bfloat16).reshape(2 * NY * rows_dev, padded_nw)
    by_cos = jnp.dot(first, cos_w, preferred_element_type=jnp.float32)
    by_sin = jnp.dot(first, sin_w, preferred_element_type=jnp.float32)
    by_cos = by_cos.reshape(rows_dev, 2, NY, padded_nw)
    by_sin = by_sin.reshape(rows_dev, 2, NY, padded_nw)
    second = jnp.stack([by_cos[:, 0] + by_sin[:, 1], by_cos[:, 1] - by_sin[:, 0]], axis=2)
    second = jnp.transpose(second, (1, 0, 2, 3))
    second = second.astype(jnp.bfloat16).reshape(devices, per_dev * rows_dev * 2, padded_nw)
    pencils = lax.all_to_all(second, ("sky", "gz"), split_axis=0, concat_axis=0, tiled=True)
    pencils = pencils.reshape(devices, per_dev, rows_dev, 2, padded_nw)[..., :NW]
    return jnp.einsum("sqxRv,RsxUu->Uuqv", pencils, table_x, preferred_element_type=jnp.float32)


def solution(mesh):
    in_specs = (P("sky", "gz"), P("sky", None), P("sky", None), P("sky"))
    out_specs = P(None, None, ("sky", "gz"), None)
    return jax.shard_map(shards, mesh=mesh, in_specs=in_specs, out_specs=out_specs, check_vma=False)
```

```python
import math

import jax
import jax.numpy as jnp
from jax import lax
from jax.sharding import PartitionSpec as P

NX = 256
NY = 256
NW = 1032
KSIDE = 4


def dft_tables(length, steps=None):
    if steps is None:
        steps = jnp.arange(length, dtype=jnp.int32)
    phase = steps[:, None] * steps[None, :] % length
    angles = phase.astype(jnp.float32) * (2.0 * math.pi / length)
    factor = 1.0 / math.sqrt(length)
    return (
        (jnp.cos(angles) * factor).astype(jnp.bfloat16),
        (jnp.sin(angles) * factor).astype(jnp.bfloat16),
    )


def twiddles(length, padded, fine_count=16):
    coarse_count = padded // fine_count
    steps = jnp.arange(padded, dtype=jnp.int32)
    angle = 2.0 * math.pi / length
    coarse = (jnp.arange(coarse_count, dtype=jnp.int32)[:, None] * fine_count * steps[None, :]) % length
    fine = (jnp.arange(fine_count, dtype=jnp.int32)[:, None] * steps[None, :]) % length
    cos_c = jnp.cos(coarse.astype(jnp.float32) * angle)[:, None, :]
    sin_c = jnp.sin(coarse.astype(jnp.float32) * angle)[:, None, :]
    cos_f = jnp.cos(fine.astype(jnp.float32) * angle)[None, :, :]
    sin_f = jnp.sin(fine.astype(jnp.float32) * angle)[None, :, :]
    cos_t = (cos_c * cos_f - sin_c * sin_f).reshape(padded, padded)
    sin_t = (sin_c * cos_f + cos_c * sin_f).reshape(padded, padded)
    inside = (steps[:, None] < length) & (steps[None, :] < length)
    factor = 1.0 / math.sqrt(length)
    cos_t = jnp.where(inside, cos_t * factor, 0.0).astype(jnp.bfloat16)
    sin_t = jnp.where(inside, sin_t * factor, 0.0).astype(jnp.bfloat16)
    return cos_t, sin_t


def complex_table(length, steps=None):
    cos_t, sin_t = dft_tables(length, steps)
    top = jnp.concatenate([cos_t, -sin_t], axis=1)
    bottom = jnp.concatenate([sin_t, cos_t], axis=1)
    return jnp.concatenate([top, bottom], axis=0)


def route_fibres(spectra, kernel, owner, offset, sky_count):
    fibre_count = spectra.shape[0]
    capacity = fibre_count * 5 // (4 * sky_count)
    block = 2 * capacity
    slots_all = sky_count * block
    target = owner[:, 0]
    order = jnp.arange(fibre_count, dtype=jnp.int32)
    same = (target[:, None] == target[None, :]) & (order[None, :] < order[:, None])
    before = jnp.sum(same.astype(jnp.int32), axis=1)
    first_slot = target * block + before
    second_slot = ((target + 1) % sky_count) * block + capacity + before
    slot_ids = jnp.arange(slots_all, dtype=jnp.int32)
    pick = (
        (slot_ids[:, None] == first_slot[None, :]) | (slot_ids[:, None] == second_slot[None, :])
    ).astype(jnp.bfloat16)
    row = (offset // NY).astype(jnp.bfloat16)[:, None]
    col = (offset % NY).astype(jnp.bfloat16)[:, None]
    packed = jnp.concatenate([spectra, kernel, row, col], axis=1)
    send = jnp.dot(pick, packed, preferred_element_type=jnp.float32).astype(jnp.bfloat16)
    send = send.reshape(sky_count, block, packed.shape[1])
    got = lax.all_to_all(send, "sky", split_axis=0, concat_axis=0, tiled=True)
    return got.reshape(slots_all, packed.shape[1]), capacity, block


def grid_rows(got, values_t, slab_width, row_ids, capacity, block):
    slots_all = got.shape[0]
    slot_ids = jnp.arange(slots_all, dtype=jnp.int32)
    shift = jnp.where(slot_ids % block >= capacity, NX // (slots_all // block), 0)
    corner_row = got[:, slab_width + KSIDE * KSIDE].astype(jnp.int32) - shift
    corner_col = got[:, slab_width + KSIDE * KSIDE + 1].astype(jnp.int32)
    columns = jnp.arange(NY, dtype=jnp.int32)
    spread = jnp.zeros((NY, row_ids.shape[0], slots_all), jnp.bfloat16)
    for step_a in range(KSIDE):
        line = jnp.zeros((NY, slots_all), jnp.bfloat16)
        for step_b in range(KSIDE):
            placed = columns[:, None] == ((corner_col + step_b) % NY)[None, :]
            tap = got[:, slab_width + step_a * KSIDE + step_b][None, :]
            line = jnp.where(placed, tap, line)
        active = row_ids[:, None] == (corner_row + step_a)[None, :]
        spread = jnp.where(active[None, :, :], line[:, None, :], spread)
    spread = spread.reshape(NY * row_ids.shape[0], slots_all)
    cube = lax.dot_general(
        spread, values_t, (((1,), (1,)), ((), ())), preferred_element_type=jnp.float32
    )
    return cube.astype(jnp.bfloat16)


def shards(spectra, kernel, owner, offset):
    sky_count = lax.axis_size("sky")
    gz_count = lax.axis_size("gz")
    devices = sky_count * gz_count
    slab_width = spectra.shape[1]
    taps = kernel.shape[1]
    tile_rows = NX // sky_count
    per_dev = NY // devices

    got, capacity, block = route_fibres(spectra, kernel, owner, offset, sky_count)
    rows_dev = tile_rows // gz_count
    padded_nw = -(-NW // 128) * 128
    values_t = jnp.transpose(got[:, :slab_width])
    copies = jnp.broadcast_to(values_t[None], (gz_count,) + values_t.shape)
    values_t = lax.all_to_all(copies, "gz", split_axis=0, concat_axis=0, tiled=True)
    values_t = jnp.pad(values_t.reshape(NW, -1), ((0, padded_nw - NW), (0, 0)))
    row_ids = lax.axis_index("gz") * rows_dev + jnp.arange(rows_dev, dtype=jnp.int32)
    cube_yw = grid_rows(got, values_t, slab_width, row_ids, capacity, block)
    cube_yw = cube_yw.reshape(NY, rows_dev, padded_nw)
    steps_y = jnp.arange(NY, dtype=jnp.int32)
    steps_x = jnp.arange(NX, dtype=jnp.int32)

    cos_y, sin_y = dft_tables(NY, steps_y)
    table_y = jnp.concatenate([cos_y, -sin_y], axis=1)
    cos_w, sin_w = twiddles(NW, padded_nw)
    table_x = complex_table(NX, steps_x).reshape(2, devices, rows_dev, 2, NX)
    table_y, cos_w, sin_w, table_x = lax.optimization_barrier((table_y, cos_w, sin_w, table_x))

    first = jnp.einsum("yxw,yK->xKw", cube_yw, table_y, preferred_element_type=jnp.float32)
    first = first.astype(jnp.bfloat16).reshape(2 * NY * rows_dev, padded_nw)
    by_cos = jnp.dot(first, cos_w, preferred_element_type=jnp.float32)
    by_sin = jnp.dot(first, sin_w, preferred_element_type=jnp.float32)
    by_cos = by_cos.reshape(rows_dev, 2, NY, padded_nw)
    by_sin = by_sin.reshape(rows_dev, 2, NY, padded_nw)
    second = jnp.stack([by_cos[:, 0] + by_sin[:, 1], by_cos[:, 1] - by_sin[:, 0]], axis=2)
    second = jnp.transpose(second, (1, 0, 2, 3))
    second = second.astype(jnp.bfloat16).reshape(devices, per_dev * rows_dev * 2, padded_nw)
    pencils = lax.all_to_all(second, ("sky", "gz"), split_axis=0, concat_axis=0, tiled=True)
    pencils = pencils.reshape(devices, per_dev, rows_dev, 2, padded_nw)[..., :NW]
    return jnp.einsum("sqxRv,RsxUu->Uuqv", pencils, table_x, preferred_element_type=jnp.float32)


def solution(mesh):
    in_specs = (P("sky", "gz"), P("sky", None), P("sky", None), P("sky"))
    out_specs = P(None, None, ("sky", "gz"), None)
    return jax.shard_map(shards, mesh=mesh, in_specs=in_specs, out_specs=out_specs, check_vma=False)
```

```python
import math

import jax
import jax.numpy as jnp
from jax import lax
from jax.sharding import PartitionSpec as P

NX = 256
NY = 256
NW = 1032
KSIDE = 4


def dft_tables(length, steps=None):
    if steps is None:
        steps = jnp.arange(length, dtype=jnp.int32)
    phase = steps[:, None] * steps[None, :] % length
    angles = phase.astype(jnp.float32) * (2.0 * math.pi / length)
    factor = 1.0 / math.sqrt(length)
    return (
        (jnp.cos(angles) * factor).astype(jnp.bfloat16),
        (jnp.sin(angles) * factor).astype(jnp.bfloat16),
    )


def twiddles(length, padded, fine_count=16):
    coarse_count = padded // fine_count
    steps = jnp.arange(padded, dtype=jnp.int32)
    angle = 2.0 * math.pi / length
    coarse = (jnp.arange(coarse_count, dtype=jnp.int32)[:, None] * fine_count * steps[None, :]) % length
    fine = (jnp.arange(fine_count, dtype=jnp.int32)[:, None] * steps[None, :]) % length
    cos_c = jnp.cos(coarse.astype(jnp.float32) * angle)[:, None, :]
    sin_c = jnp.sin(coarse.astype(jnp.float32) * angle)[:, None, :]
    cos_f = jnp.cos(fine.astype(jnp.float32) * angle)[None, :, :]
    sin_f = jnp.sin(fine.astype(jnp.float32) * angle)[None, :, :]
    cos_t = (cos_c * cos_f - sin_c * sin_f).reshape(padded, padded)
    sin_t = (sin_c * cos_f + cos_c * sin_f).reshape(padded, padded)
    inside = (steps[:, None] < length) & (steps[None, :] < length)
    factor = 1.0 / math.sqrt(length)
    cos_t = jnp.where(inside, cos_t * factor, 0.0).astype(jnp.bfloat16)
    sin_t = jnp.where(inside, sin_t * factor, 0.0).astype(jnp.bfloat16)
    return cos_t, sin_t


def complex_table(length, steps=None):
    cos_t, sin_t = dft_tables(length, steps)
    top = jnp.concatenate([cos_t, -sin_t], axis=1)
    bottom = jnp.concatenate([sin_t, cos_t], axis=1)
    return jnp.concatenate([top, bottom], axis=0)


def route_fibres(spectra, kernel, owner, offset, sky_count):
    fibre_count = spectra.shape[0]
    capacity = fibre_count * 5 // (4 * sky_count)
    block = 2 * capacity
    slots_all = sky_count * block
    target = owner[:, 0]
    order = jnp.arange(fibre_count, dtype=jnp.int32)
    same = (target[:, None] == target[None, :]) & (order[None, :] < order[:, None])
    before = jnp.sum(same.astype(jnp.int32), axis=1)
    first_slot = target * block + before
    second_slot = ((target + 1) % sky_count) * block + capacity + before
    slot_ids = jnp.arange(slots_all, dtype=jnp.int32)
    pick = (
        (slot_ids[:, None] == first_slot[None, :]) | (slot_ids[:, None] == second_slot[None, :])
    ).astype(jnp.bfloat16)
    row = (offset // NY).astype(jnp.bfloat16)[:, None]
    col = (offset % NY).astype(jnp.bfloat16)[:, None]
    packed = jnp.concatenate([spectra, kernel, row, col], axis=1)
    send = jnp.dot(pick, packed, preferred_element_type=jnp.float32).astype(jnp.bfloat16)
    send = send.reshape(sky_count, block, packed.shape[1])
    got = lax.all_to_all(send, "sky", split_axis=0, concat_axis=0, tiled=True)
    return got.reshape(slots_all, packed.shape[1]), capacity, block


def grid_rows(got, values_t, slab_width, row_ids, capacity, block):
    slots_all = got.shape[0]
    slot_ids = jnp.arange(slots_all, dtype=jnp.int32)
    shift = jnp.where(slot_ids % block >= capacity, NX // (slots_all // block), 0)
    corner_row = got[:, slab_width + KSIDE * KSIDE].astype(jnp.int32) - shift
    corner_col = got[:, slab_width + KSIDE * KSIDE + 1].astype(jnp.int32)
    columns = jnp.arange(NY, dtype=jnp.int32)
    spread = jnp.zeros((NY, row_ids.shape[0], slots_all), jnp.bfloat16)
    for step_a in range(KSIDE):
        line = jnp.zeros((NY, slots_all), jnp.bfloat16)
        for step_b in range(KSIDE):
            placed = columns[:, None] == ((corner_col + step_b) % NY)[None, :]
            tap = got[:, slab_width + step_a * KSIDE + step_b][None, :]
            line = jnp.where(placed, tap, line)
        active = row_ids[:, None] == (corner_row + step_a)[None, :]
        spread = jnp.where(active[None, :, :], line[:, None, :], spread)
    spread = spread.reshape(NY * row_ids.shape[0], slots_all)
    cube = lax.dot_general(
        spread, values_t, (((1,), (1,)), ((), ())), preferred_element_type=jnp.float32
    )
    return cube.astype(jnp.bfloat16)


def shards(spectra, kernel, owner, offset):
    sky_count = lax.axis_size("sky")
    gz_count = lax.axis_size("gz")
    devices = sky_count * gz_count
    slab_width = spectra.shape[1]
    taps = kernel.shape[1]
    tile_rows = NX // sky_count
    per_dev = NY // devices

    got, capacity, block = route_fibres(spectra, kernel, owner, offset, sky_count)
    rows_dev = tile_rows // gz_count
    padded_nw = -(-NW // 128) * 128
    values_t = jnp.transpose(got[:, :slab_width])
    copies = jnp.broadcast_to(values_t[None], (gz_count,) + values_t.shape)
    steps_y = jnp.arange(NY, dtype=jnp.int32)
    steps_x = jnp.arange(NX, dtype=jnp.int32)
    copies, steps_y, steps_x = lax.optimization_barrier((copies, steps_y, steps_x))
    values_t = lax.all_to_all(copies, "gz", split_axis=0, concat_axis=0, tiled=True)
    values_t = jnp.pad(values_t.reshape(NW, -1), ((0, padded_nw - NW), (0, 0)))
    row_ids = lax.axis_index("gz") * rows_dev + jnp.arange(rows_dev, dtype=jnp.int32)
    cube_yw = grid_rows(got, values_t, slab_width, row_ids, capacity, block)
    cube_yw = cube_yw.reshape(NY, rows_dev, padded_nw)

    cos_y, sin_y = dft_tables(NY, steps_y)
    table_y = jnp.concatenate([cos_y, -sin_y], axis=1)
    cos_w, sin_w = twiddles(NW, padded_nw)
    table_x = complex_table(NX, steps_x).reshape(2, devices, rows_dev, 2, NX)
    table_y, cos_w, sin_w, table_x = lax.optimization_barrier((table_y, cos_w, sin_w, table_x))

    first = jnp.einsum("yxw,yK->xKw", cube_yw, table_y, preferred_element_type=jnp.float32)
    first = first.astype(jnp.bfloat16).reshape(2 * NY * rows_dev, padded_nw)
    by_cos = jnp.dot(first, cos_w, preferred_element_type=jnp.float32)
    by_sin = jnp.dot(first, sin_w, preferred_element_type=jnp.float32)
    by_cos = by_cos.reshape(rows_dev, 2, NY, padded_nw)
    by_sin = by_sin.reshape(rows_dev, 2, NY, padded_nw)
    second = jnp.stack([by_cos[:, 0] + by_sin[:, 1], by_cos[:, 1] - by_sin[:, 0]], axis=2)
    second = jnp.transpose(second, (1, 0, 2, 3))
    second = second.astype(jnp.bfloat16).reshape(devices, per_dev * rows_dev * 2, padded_nw)
    pencils = lax.all_to_all(second, ("sky", "gz"), split_axis=0, concat_axis=0, tiled=True)
    pencils = pencils.reshape(devices, per_dev, rows_dev, 2, padded_nw)[..., :NW]
    return jnp.einsum("sqxRv,RsxUu->Uuqv", pencils, table_x, preferred_element_type=jnp.float32)


def solution(mesh):
    in_specs = (P("sky", "gz"), P("sky", None), P("sky", None), P("sky"))
    out_specs = P(None, None, ("sky", "gz"), None)
    return jax.shard_map(shards, mesh=mesh, in_specs=in_specs, out_specs=out_specs, check_vma=False)
```

```python
import math

import jax
import jax.numpy as jnp
from jax import lax
from jax.sharding import PartitionSpec as P

NX = 256
NY = 256
NW = 1032
KSIDE = 4


def passed_along(block, axis, distance):
    devices = range(lax.axis_size(axis))
    route = [((i - distance) % len(devices), i) for i in devices]
    return lax.ppermute(block, axis, route)


def dft_tables(length, steps=None):
    if steps is None:
        steps = jnp.arange(length, dtype=jnp.int32)
    phase = steps[:, None] * steps[None, :] % length
    angles = phase.astype(jnp.float32) * (2.0 * math.pi / length)
    factor = 1.0 / math.sqrt(length)
    return (
        (jnp.cos(angles) * factor).astype(jnp.bfloat16),
        (jnp.sin(angles) * factor).astype(jnp.bfloat16),
    )


def twiddles(length, padded, fine_count=16):
    coarse_count = padded // fine_count
    steps = jnp.arange(padded, dtype=jnp.int32)
    angle = 2.0 * math.pi / length
    coarse = (jnp.arange(coarse_count, dtype=jnp.int32)[:, None] * fine_count * steps[None, :]) % length
    fine = (jnp.arange(fine_count, dtype=jnp.int32)[:, None] * steps[None, :]) % length
    cos_c = jnp.cos(coarse.astype(jnp.float32) * angle)[:, None, :]
    sin_c = jnp.sin(coarse.astype(jnp.float32) * angle)[:, None, :]
    cos_f = jnp.cos(fine.astype(jnp.float32) * angle)[None, :, :]
    sin_f = jnp.sin(fine.astype(jnp.float32) * angle)[None, :, :]
    cos_t = (cos_c * cos_f - sin_c * sin_f).reshape(padded, padded)
    sin_t = (sin_c * cos_f + cos_c * sin_f).reshape(padded, padded)
    inside = (steps[:, None] < length) & (steps[None, :] < length)
    factor = 1.0 / math.sqrt(length)
    cos_t = jnp.where(inside, cos_t * factor, 0.0).astype(jnp.bfloat16)
    sin_t = jnp.where(inside, sin_t * factor, 0.0).astype(jnp.bfloat16)
    return cos_t, sin_t


def complex_table(length, steps=None):
    cos_t, sin_t = dft_tables(length, steps)
    top = jnp.concatenate([cos_t, -sin_t], axis=1)
    bottom = jnp.concatenate([sin_t, cos_t], axis=1)
    return jnp.concatenate([top, bottom], axis=0)


def route_fibres(spectra, kernel, owner, offset, sky_count):
    fibre_count = spectra.shape[0]
    capacity = fibre_count * 5 // (4 * sky_count)
    block = 2 * capacity
    slots_all = sky_count * block
    target = owner[:, 0]
    order = jnp.arange(fibre_count, dtype=jnp.int32)
    same = (target[:, None] == target[None, :]) & (order[None, :] < order[:, None])
    before = jnp.sum(same.astype(jnp.int32), axis=1)
    first_slot = target * block + before
    second_slot = ((target + 1) % sky_count) * block + capacity + before
    slot_ids = jnp.arange(slots_all, dtype=jnp.int32)
    pick = (
        (slot_ids[:, None] == first_slot[None, :]) | (slot_ids[:, None] == second_slot[None, :])
    ).astype(jnp.bfloat16)
    row = (offset // NY).astype(jnp.bfloat16)[:, None]
    col = (offset % NY).astype(jnp.bfloat16)[:, None]
    packed = jnp.concatenate([spectra, kernel, row, col], axis=1)
    send = jnp.dot(pick, packed, preferred_element_type=jnp.float32).astype(jnp.bfloat16)
    send = send.reshape(sky_count, block, packed.shape[1])
    got = lax.all_to_all(send, "sky", split_axis=0, concat_axis=0, tiled=True)
    return got.reshape(slots_all, packed.shape[1]), capacity, block


def grid_rows(got, values_t, slab_width, row_ids, capacity, block):
    slots_all = got.shape[0]
    slot_ids = jnp.arange(slots_all, dtype=jnp.int32)
    shift = jnp.where(slot_ids % block >= capacity, NX // (slots_all // block), 0)
    corner_row = got[:, slab_width + KSIDE * KSIDE].astype(jnp.int32) - shift
    corner_col = got[:, slab_width + KSIDE * KSIDE + 1].astype(jnp.int32)
    columns = jnp.arange(NY, dtype=jnp.int32)
    spread = jnp.zeros((NY, row_ids.shape[0], slots_all), jnp.bfloat16)
    for step_a in range(KSIDE):
        line = jnp.zeros((NY, slots_all), jnp.bfloat16)
        for step_b in range(KSIDE):
            placed = columns[:, None] == ((corner_col + step_b) % NY)[None, :]
            tap = got[:, slab_width + step_a * KSIDE + step_b][None, :]
            line = jnp.where(placed, tap, line)
        active = row_ids[:, None] == (corner_row + step_a)[None, :]
        spread = jnp.where(active[None, :, :], line[:, None, :], spread)
    spread = spread.reshape(NY * row_ids.shape[0], slots_all)
    cube = lax.dot_general(
        spread, values_t, (((1,), (1,)), ((), ())), preferred_element_type=jnp.float32
    )
    return cube.astype(jnp.bfloat16)


def shards(spectra, kernel, owner, offset):
    sky_count = lax.axis_size("sky")
    gz_count = lax.axis_size("gz")
    devices = sky_count * gz_count
    slab_width = spectra.shape[1]
    taps = kernel.shape[1]
    tile_rows = NX // sky_count
    per_dev = NY // devices

    got, capacity, block = route_fibres(spectra, kernel, owner, offset, sky_count)
    rows_dev = tile_rows // gz_count
    padded_nw = -(-NW // 128) * 128
    values_t = jnp.transpose(got[:, :slab_width])
    steps_y = jnp.arange(NY, dtype=jnp.int32)
    steps_x = jnp.arange(NX, dtype=jnp.int32)
    values_t, steps_y, steps_x = lax.optimization_barrier((values_t, steps_y, steps_x))
    held = [values_t] + [passed_along(values_t, "gz", d) for d in range(1, gz_count)]
    held = jnp.stack(held[::-1])
    start = (-(lax.axis_index("gz") + 1)) % gz_count
    doubled = jnp.concatenate([held, held], axis=0)
    values_t = lax.dynamic_slice_in_dim(doubled, start, gz_count, axis=0)
    values_t = jnp.pad(values_t.reshape(NW, -1), ((0, padded_nw - NW), (0, 0)))
    row_ids = lax.axis_index("gz") * rows_dev + jnp.arange(rows_dev, dtype=jnp.int32)
    cube_yw = grid_rows(got, values_t, slab_width, row_ids, capacity, block)
    cube_yw = cube_yw.reshape(NY, rows_dev, padded_nw)

    cos_y, sin_y = dft_tables(NY, steps_y)
    table_y = jnp.concatenate([cos_y, -sin_y], axis=1)
    cos_w, sin_w = twiddles(NW, padded_nw)
    table_x = complex_table(NX, steps_x).reshape(2, devices, rows_dev, 2, NX)
    table_y, cos_w, sin_w, table_x = lax.optimization_barrier((table_y, cos_w, sin_w, table_x))

    first = jnp.einsum("yxw,yK->xKw", cube_yw, table_y, preferred_element_type=jnp.float32)
    first = first.astype(jnp.bfloat16).reshape(2 * NY * rows_dev, padded_nw)
    by_cos = jnp.dot(first, cos_w, preferred_element_type=jnp.float32)
    by_sin = jnp.dot(first, sin_w, preferred_element_type=jnp.float32)
    by_cos = by_cos.reshape(rows_dev, 2, NY, padded_nw)
    by_sin = by_sin.reshape(rows_dev, 2, NY, padded_nw)
    second = jnp.stack([by_cos[:, 0] + by_sin[:, 1], by_cos[:, 1] - by_sin[:, 0]], axis=2)
    second = jnp.transpose(second, (1, 0, 2, 3))
    second = second.astype(jnp.bfloat16).reshape(devices, per_dev * rows_dev * 2, padded_nw)
    pencils = lax.all_to_all(second, ("sky", "gz"), split_axis=0, concat_axis=0, tiled=True)
    pencils = pencils.reshape(devices, per_dev, rows_dev, 2, padded_nw)[..., :NW]
    return jnp.einsum("sqxRv,RsxUu->Uuqv", pencils, table_x, preferred_element_type=jnp.float32)


def solution(mesh):
    in_specs = (P("sky", "gz"), P("sky", None), P("sky", None), P("sky"))
    out_specs = P(None, None, ("sky", "gz"), None)
    return jax.shard_map(shards, mesh=mesh, in_specs=in_specs, out_specs=out_specs, check_vma=False)
```
